128 devices in a mesh: member: 4 (over x_lo, core), band: 32 (over y, z, x_hi).
Axes of the slice: x: 4 (x_hi: 2, x_lo: 2; x = x_hi * 2 + x_lo), y: 4, z: 4, core: 2. Of those that a mesh axis runs over, the one named last changes fastest.
Arguments:
- parent_state: float32 [32, 3, 512, 4096], P('member', None, 'band'), parts along dimension 0, may hold values from -6 to 6
- nest_state: float32 [32, 3, 768, 768], P('member', None, 'band'), parts along dimension 0, may hold values from -6 to 6
- offsets: int32 [32, 2], P('member'), parts along dimension 0, may hold values from 2 to 3838, as said below
Outputs:
- parent_out: float32 [32, 3, 512, 4096], P('member', None, 'band'), parts along dimension 0
- nest_out: float32 [32, 3, 768, 768], P('member', None, 'band'), parts along dimension 0
The draws below stay inside these ranges and needn't reach their ends.
There are 4 independent parts, one for each index of `member`. The reference program is written for one: setup_inputs(seed, part) draws one part's arguments, and reference() takes and returns one part's arrays. A program takes and returns all parts, laid end to end along the dimension named above; each array names one. Nothing has to cross between parts.
Inputs may be any that keep to these rules, and one draw needn't show every extreme that they name: Column 0 holds row offsets from 2 to 254, column 1 column offsets from 2 to 3838; in each column some member takes the lowest and some member the highest of its range.
All inputs are finite; a program needn't handle non-finite values.
Results may differ from the reference program's by a relative error of at most 0.00012.
Values sent between devices are 32-bit elements; how exact they have to be, the bound alone decides.
No kernel may reach another device: no remote copies, remote signals or barrier semaphores. Data moves between devices by JAX's collectives and lax.ppermute only.
A program may use at most 256 MiB of HBM per device.

```python
import jax
import jax.numpy as jnp
from jax import lax

MEMB = 8
NX = 4096
NSTEPS = 3
NY = 512
NN = 768
NC = 256


def draw_offsets(key, part):
    keys = jax.random.split(jax.random.fold_in(key, 11), 4)
    row_top = NY - NC - 2
    col_top = NX - NC - 2
    rows = jax.random.randint(keys[0], (MEMB,), 2, row_top + 1)
    rows = rows.at[0].set(2).at[1].set(row_top)
    rows = jax.random.permutation(keys[1], rows)
    cols = jax.random.randint(keys[2], (MEMB,), 2, col_top + 1)
    cols = cols.at[0].set(2).at[1].set(col_top)
    cols = jax.random.permutation(keys[3], cols)
    return jnp.stack([rows, cols], axis=1).astype(jnp.int32)


def block_levels(own_key, dims, cuts, least, top_value):
    def one(position, blocks):
        steps = jax.random.uniform(jax.random.fold_in(jax.random.fold_in(own_key, 6), position), (blocks,), jnp.float32, least / len(cuts), top_value / len(cuts))
        return jnp.repeat(jnp.exp(steps), dims[position] // blocks).reshape((-1,) + (1,) * (len(dims) - position - 1))

    level = one(*cuts[0])
    for cut in cuts[1:]:
        level = level * one(*cut)
    return level


def centred(rng, dims, deviation, limit, shards=(), kind=jnp.bfloat16):
    values = jax.random.normal(rng, dims, jnp.float32) * deviation
    if len(shards) > 0:
        values = block_levels(rng, dims, shards, -0.22, 0.18) * values
    return jnp.clip(values, min=-limit, max=limit).astype(kind)


def setup_inputs(seed: int = 0, part: int = 0) -> dict:
    seeds = jax.random.split(jax.random.key(seed), 4)
    part_splits = jax.random.split(jax.random.fold_in(seeds[3], part), 4)
    parent_state = centred(part_splits[0], (MEMB, 3, NY, NX), 1.0, 6.0, ((2, 32),), jnp.float32)
    nest_state = centred(part_splits[1], (MEMB, 3, NN, NN), 1.0, 6.0, ((2, 32),), jnp.float32)
    offsets = draw_offsets(jax.random.fold_in(jax.random.fold_in(seeds[3], part), 71), part)
    return {"parent_state": parent_state, "nest_state": nest_state, "offsets": offsets}


courant = 0.9
friction = 0.02
rotation = 0.05
highest = lax.Precision.HIGHEST


def interp_matrix(fine, coarse_count):
    rows = jnp.arange(fine, dtype=jnp.int32)[:, None] + 1
    cols = jnp.arange(coarse_count, dtype=jnp.int32)[None, :]
    base = rows // 3
    frac = rows % 3
    upper = frac.astype(jnp.float32) / 3.0
    lower = (3 - frac).astype(jnp.float32) / 3.0
    return jnp.where(cols == base, lower, 0.0) + jnp.where(cols == base + 1, upper, 0.0)


def shift_cols(field):
    return 0.5 * (jnp.roll(field, -1, axis=-1) - jnp.roll(field, 1, axis=-1))


def shift_rows(field):
    padded = jnp.pad(field, ((0, 0), (1, 1), (0, 0)))
    return 0.5 * (padded[:, 2:] - padded[:, :-2])


def parent_step(state):
    height, zonal, meridional = state[:, 0], state[:, 1], state[:, 2]
    height_new = height - courant * (shift_cols(zonal) + shift_rows(meridional))
    zonal_new = (1.0 - friction) * zonal - courant * shift_cols(height_new) + rotation * meridional
    merid_new = (1.0 - friction) * meridional - courant * shift_rows(height_new) - rotation * zonal
    return jnp.stack([height_new, zonal_new, merid_new], axis=1)


def embed(inner, loop):
    return loop.at[:, :, 1:-1, 1:-1].set(inner)


def nest_step(state, loop):
    height, zonal, meridional = state[:, 0], state[:, 1], state[:, 2]
    flows = embed(state[:, 1:3], loop[:, 1:3])
    height_new = height - courant * (0.5 * (flows[:, 0, 1:-1, 2:] - flows[:, 0, 1:-1, :-2]) + 0.5 * (flows[:, 1, 2:, 1:-1] - flows[:, 1, :-2, 1:-1]))
    padded = embed(height_new[:, None], loop[:, 0:1])[:, 0]
    zonal_new = (1.0 - friction) * zonal - courant * (0.5 * (padded[:, 1:-1, 2:] - padded[:, 1:-1, :-2])) + rotation * meridional
    merid_new = (1.0 - friction) * meridional - courant * (0.5 * (padded[:, 2:, 1:-1] - padded[:, :-2, 1:-1])) - rotation * zonal
    return jnp.stack([height_new, zonal_new, merid_new], axis=1)


def reference(parent_state, nest_state, offsets):
    members = parent_state.shape[0]
    stepped = parent_step(parent_state)
    rows_off = offsets[:, 0].astype(jnp.int32)
    cols_off = offsets[:, 1].astype(jnp.int32)
    zero_index = jnp.zeros((), jnp.int32)

    def window(field, row0, col0):
        return lax.dynamic_slice(field, (zero_index, row0 - 1, col0 - 1), (3, NC + 2, NC + 2))

    windows = jax.vmap(window)(stepped, rows_off, cols_off)
    weights = interp_matrix(NN + 2, NC + 2)
    along = jnp.einsum('ip,mfpq->mfiq', weights, windows, precision=highest)
    loop = jnp.einsum('mfiq,jq->mfij', along, weights, precision=highest)
    nest = nest_state
    for _ in range(NSTEPS):
        nest = nest_step(nest, loop)
    coarse = nest.reshape(members, 3, NC, 3, NC, 3).mean(axis=(3, 5))

    def put(field, patch, row0, col0):
        return lax.dynamic_update_slice(field, patch, (zero_index, row0, col0))

    parent_out = jax.vmap(put)(stepped, coarse, rows_off, cols_off)
    return parent_out, nest
```

```python
import jax
import jax.numpy as jnp
from jax import lax
from jax.sharding import PartitionSpec as P

NSTEPS = 3


courant = 0.9
friction = 0.02
rotation = 0.05
highest = lax.Precision.HIGHEST


def shift_pairs(count, shift):
    if shift > 0:
        return [(i, i + shift) for i in range(count - shift)]
    return [(i, i + shift) for i in range(-shift, count)]


def with_halo(cells, width):
    count = lax.axis_size("band")
    head = cells[:, :, :width]
    tail = cells[:, :, cells.shape[2] - width :]
    return jnp.concatenate(
        [
            lax.ppermute(tail, "band", shift_pairs(count, 1)),
            cells,
            lax.ppermute(head, "band", shift_pairs(count, -1)),
        ],
        axis=2,
    )


def interp_matrix(fine, coarse_count):
    rows = jnp.arange(fine, dtype=jnp.int32)[:, None] + 1
    cols = jnp.arange(coarse_count, dtype=jnp.int32)[None, :]
    base = rows // 3
    frac = rows % 3
    upper = frac.astype(jnp.float32) / 3.0
    lower = (3 - frac).astype(jnp.float32) / 3.0
    return jnp.where(cols == base, lower, 0.0) + jnp.where(cols == base + 1, upper, 0.0)


def shift_cols(field):
    return 0.5 * (jnp.roll(field, -1, axis=-1) - jnp.roll(field, 1, axis=-1))


def parent_step(parent_state):
    height, zonal, meridional = (parent_state[:, 0], parent_state[:, 1], parent_state[:, 2])
    merid_ext = with_halo(meridional[:, None], 1)[:, 0]
    height_new = height - courant * (
        shift_cols(zonal) + 0.5 * (merid_ext[:, 2:] - merid_ext[:, :-2])
    )
    height_ext = with_halo(height_new[:, None], 1)[:, 0]
    zonal_new = (1.0 - friction) * zonal - courant * shift_cols(height_new) + rotation * meridional
    merid_new = (
        (1.0 - friction) * meridional
        - courant * (0.5 * (height_ext[:, 2:] - height_ext[:, :-2]))
        - rotation * zonal
    )
    return jnp.stack([height_new, zonal_new, merid_new], axis=1)


def per_device(parent_state, nest_state, offsets):
    members = parent_state.shape[0]
    band_rows = parent_state.shape[2]
    nest_rows = nest_state.shape[2]
    nest_width = nest_state.shape[3]
    span = nest_width // 3
    tile_coarse = nest_rows // 3
    bands = lax.axis_size("band")
    band_index = lax.axis_index("band")
    parent_total = bands * band_rows
    nest_total = bands * nest_rows
    halo = 2 * NSTEPS
    ext_rows = nest_rows + 2 * halo
    rows_off = offsets[:, 0]
    cols_off = offsets[:, 1]
    two = jnp.float32(2.0) / jnp.float32(3.0)
    one = jnp.float32(1.0) / jnp.float32(3.0)

    stepped = parent_step(parent_state)

    colslice = jax.vmap(lambda f, c0: lax.dynamic_slice_in_dim(f, c0 - 1, span + 2, axis=2))(
        stepped, cols_off
    )

    west = two * colslice[..., 0] + one * colslice[..., 1]
    east = one * colslice[..., span] + two * colslice[..., span + 1]
    strip = jnp.stack([west, east], axis=2)
    gathered = lax.all_gather(strip.reshape(1, -1), "band", axis=0, tiled=True)
    strip_all = (
        gathered.reshape(bands, members, 3, 2, band_rows)
        .transpose(1, 2, 3, 0, 4)
        .reshape(members, 3, 2, parent_total)
    )

    global_rows = band_index * band_rows + jnp.arange(band_rows, dtype=jnp.int32)
    row_start = rows_off[:, None]
    south_weight = jnp.where(global_rows[None, :] == row_start - 1, two, 0.0) + jnp.where(
        global_rows[None, :] == row_start, one, 0.0
    )
    north_weight = jnp.where(global_rows[None, :] == row_start + span - 1, one, 0.0) + jnp.where(
        global_rows[None, :] == row_start + span, two, 0.0
    )
    row_weights = jnp.stack([south_weight, north_weight], axis=1)
    ends_part = jnp.einsum("msl,mflq->mfsq", row_weights, colslice, precision=highest)
    ends_full = lax.psum(ends_part, "band")
    inner_weights = interp_matrix(nest_width + 2, span + 2)[1:-1]
    ends = jnp.einsum("jq,mfsq->mfsj", inner_weights, ends_full, precision=highest)

    nest_global = band_index * nest_rows - halo + jnp.arange(ext_rows, dtype=jnp.int32)
    base = (nest_global + 2) // 3
    frac = (nest_global + 2) % 3
    lower = (3 - frac).astype(jnp.float32) / 3.0
    upper = frac.astype(jnp.float32) / 3.0
    first_row = rows_off[:, None] - 1 + base[None, :]
    all_rows = jnp.arange(parent_total, dtype=jnp.int32)[None, None, :]
    side_weights = jnp.where(all_rows == first_row[:, :, None], lower[None, :, None], 0.0) + jnp.where(
        all_rows == first_row[:, :, None] + 1, upper[None, :, None], 0.0
    )
    side_ext = jnp.einsum("mkr,mfsr->mfsk", side_weights, strip_all, precision=highest)

    nest_ext = with_halo(nest_state, halo)
    is_south = (nest_global == -1)[None, :, None]
    is_north = (nest_global == nest_total)[None, :, None]

    def fix(field, f):
        return jnp.where(
            is_south,
            ends[:, f, 0][:, None, :],
            jnp.where(is_north, ends[:, f, 1][:, None, :], field),
        )

    def dx(field, f):
        west_col = side_ext[:, f, 0][:, :, None]
        east_col = side_ext[:, f, 1][:, :, None]
        right = jnp.concatenate([field[:, :, 1:], east_col], axis=2)
        left = jnp.concatenate([west_col, field[:, :, :-1]], axis=2)
        return 0.5 * (right - left)

    def dy(field):
        zero = jnp.zeros_like(field[:, :1])
        up = jnp.concatenate([field[:, 1:], zero], axis=1)
        down = jnp.concatenate([zero, field[:, :-1]], axis=1)
        return 0.5 * (up - down)

    height, zonal, meridional = (nest_ext[:, 0], nest_ext[:, 1], nest_ext[:, 2])
    for _ in range(NSTEPS):
        zonal_fixed = fix(zonal, 1)
        merid_fixed = fix(meridional, 2)
        height_new = height - courant * (dx(zonal_fixed, 1) + dy(merid_fixed))
        height_fixed = fix(height_new, 0)
        zonal_new = (1.0 - friction) * zonal - courant * dx(height_fixed, 0) + rotation * meridional
        merid_new = (1.0 - friction) * meridional - courant * dy(height_fixed) - rotation * zonal
        height, zonal, meridional = height_new, zonal_new, merid_new
    nest = jnp.stack([height, zonal, meridional], axis=1)[:, :, halo : halo + nest_rows]

    block_cols = (
        jnp.arange(nest_width, dtype=jnp.int32)[:, None] // 3
        == jnp.arange(span, dtype=jnp.int32)[None, :]
    ).astype(jnp.float32)
    col_sums = jnp.einsum("mfrj,jp->mfrp", nest, block_cols, precision=highest)
    coarse = col_sums.reshape(members, 3, tile_coarse, 3, span).sum(axis=3) / 9.0

    shift = (rows_off + tile_coarse - 1) // tile_coarse - 1
    moved = coarse
    step = 1
    while step < bands:
        recv = lax.ppermute(moved, "band", [(i, (i + step) % bands) for i in range(bands)])
        take = ((shift // step) % 2 == 1)[:, None, None, None]
        moved = jnp.where(take, recv, moved)
        step *= 2
    half = bands // 2
    low_half = band_index < half
    pieces = []
    for i in range(3):
        got = []
        for h in range(2):
            pairs = [((2 * p - 1 + i) % bands, p) for p in range(h * half, (h + 1) * half)]
            got.append(lax.ppermute(moved, "band", pairs))
        pieces.append(jnp.where(low_half, got[0], got[1]))
    near = jnp.concatenate(pieces, axis=2)
    lead = tile_coarse * (shift + 1) - rows_off
    patch = jax.vmap(lambda blk, e: lax.dynamic_slice_in_dim(blk, e, band_rows, axis=1))(near, lead)

    relative_rows = global_rows[None, :] - rows_off[:, None]
    covered = (relative_rows >= 0) & (relative_rows < span)
    parent_out = stepped
    for m in range(members):
        start = (m, 0, 0, cols_off[m])
        current = lax.dynamic_slice(parent_out, start, (1, 3, band_rows, span))
        merged = jnp.where(covered[m][None, None, :, None], patch[m : m + 1], current)
        parent_out = lax.dynamic_update_slice(parent_out, merged, start)
    return (parent_out, nest)


def solution(mesh):
    in_specs = (P("member", None, "band", None), P("member", None, "band", None), P("member", None))
    out_specs = (P("member", None, "band", None), P("member", None, "band", None))
    return jax.shard_map(
        per_device, mesh=mesh, in_specs=in_specs, out_specs=out_specs, check_vma=False
    )
```

```python
import jax
import jax.numpy as jnp
from jax import lax
from jax.sharding import PartitionSpec as P

NSTEPS = 3


courant = 0.9
friction = 0.02
rotation = 0.05
highest = lax.Precision.HIGHEST


def shift_pairs(count, shift):
    if shift > 0:
        return [(i, i + shift) for i in range(count - shift)]
    return [(i, i + shift) for i in range(-shift, count)]


def with_halo(cells, width):
    count = lax.axis_size("band")
    head = cells[:, :, :width]
    tail = cells[:, :, cells.shape[2] - width :]
    return jnp.concatenate(
        [
            lax.ppermute(tail, "band", shift_pairs(count, 1)),
            cells,
            lax.ppermute(head, "band", shift_pairs(count, -1)),
        ],
        axis=2,
    )


def interp_matrix(fine, coarse_count):
    rows = jnp.arange(fine, dtype=jnp.int32)[:, None] + 1
    cols = jnp.arange(coarse_count, dtype=jnp.int32)[None, :]
    base = rows // 3
    frac = rows % 3
    upper = frac.astype(jnp.float32) / 3.0
    lower = (3 - frac).astype(jnp.float32) / 3.0
    return jnp.where(cols == base, lower, 0.0) + jnp.where(cols == base + 1, upper, 0.0)


def shift_cols(field):
    return 0.5 * (jnp.roll(field, -1, axis=-1) - jnp.roll(field, 1, axis=-1))


def parent_step(parent_state):
    height, zonal, meridional = (parent_state[:, 0], parent_state[:, 1], parent_state[:, 2])
    merid_ext = with_halo(meridional[:, None], 1)[:, 0]
    height_new = height - courant * (
        shift_cols(zonal) + 0.5 * (merid_ext[:, 2:] - merid_ext[:, :-2])
    )
    height_ext = with_halo(height_new[:, None], 1)[:, 0]
    zonal_new = (1.0 - friction) * zonal - courant * shift_cols(height_new) + rotation * meridional
    merid_new = (
        (1.0 - friction) * meridional
        - courant * (0.5 * (height_ext[:, 2:] - height_ext[:, :-2]))
        - rotation * zonal
    )
    return jnp.stack([height_new, zonal_new, merid_new], axis=1)


def per_device(parent_state, nest_state, offsets):
    members = parent_state.shape[0]
    band_rows = parent_state.shape[2]
    nest_rows = nest_state.shape[2]
    nest_width = nest_state.shape[3]
    span = nest_width // 3
    tile_coarse = nest_rows // 3
    bands = lax.axis_size("band")
    band_index = lax.axis_index("band")
    parent_total = bands * band_rows
    nest_total = bands * nest_rows
    halo = 2 * NSTEPS
    ext_rows = nest_rows + 2 * halo
    rows_off = offsets[:, 0]
    cols_off = offsets[:, 1]
    two = jnp.float32(2.0) / jnp.float32(3.0)
    one = jnp.float32(1.0) / jnp.float32(3.0)

    stepped = parent_step(parent_state)

    colslice = jnp.concatenate(
        [
            lax.dynamic_slice(stepped, (m, 0, 0, cols_off[m] - 1), (1, 3, band_rows, span + 2))
            for m in range(members)
        ],
        axis=0,
    )

    west = two * colslice[..., 0] + one * colslice[..., 1]
    east = one * colslice[..., span] + two * colslice[..., span + 1]
    strip = jnp.stack([west, east], axis=2).reshape(members * 6, band_rows)

    global_rows = band_index * band_rows + jnp.arange(band_rows, dtype=jnp.int32)
    row_start = rows_off[:, None]
    south_weight = jnp.where(global_rows[None, :] == row_start - 1, two, 0.0) + jnp.where(
        global_rows[None, :] == row_start, one, 0.0
    )
    north_weight = jnp.where(global_rows[None, :] == row_start + span - 1, one, 0.0) + jnp.where(
        global_rows[None, :] == row_start + span, two, 0.0
    )
    row_weights = jnp.stack([south_weight, north_weight], axis=1)
    ends_part = jnp.einsum("msl,mflq->mfsq", row_weights, colslice, precision=highest)

    blocks = strip
    sums = ends_part.reshape(members * 6, span + 2)
    reach = 1
    while reach < bands:
        count = min(4, bands // reach)
        payload = jnp.concatenate([blocks, sums], axis=1)
        width = blocks.shape[1]
        recvs = [
            lax.ppermute(payload, "band", [(i, (i + k * reach) % bands) for i in range(bands)])
            for k in range(count - 1, 0, -1)
        ]
        blocks = jnp.concatenate([got[:, :width] for got in recvs] + [blocks], axis=1)
        for got in recvs:
            sums = sums + got[:, width:]
        reach *= count
    strip_all = blocks.reshape(members, 3, 2, parent_total)
    held_rows = ((band_index + 1) * band_rows + jnp.arange(parent_total, dtype=jnp.int32)) % parent_total
    ends_full = sums.reshape(members, 3, 2, span + 2)
    inner_weights = interp_matrix(nest_width + 2, span + 2)[1:-1]
    ends = jnp.einsum("jq,mfsq->mfsj", inner_weights, ends_full, precision=highest)

    nest_global = band_index * nest_rows - halo + jnp.arange(ext_rows, dtype=jnp.int32)
    base = (nest_global + 2) // 3
    frac = (nest_global + 2) % 3
    lower = (3 - frac).astype(jnp.float32) / 3.0
    upper = frac.astype(jnp.float32) / 3.0
    first_row = rows_off[:, None] - 1 + base[None, :]
    all_rows = held_rows[None, None, :]
    side_weights = jnp.where(all_rows == first_row[:, :, None], lower[None, :, None], 0.0) + jnp.where(
        all_rows == first_row[:, :, None] + 1, upper[None, :, None], 0.0
    )
    side_ext = jnp.einsum("mkr,mfsr->mfsk", side_weights, strip_all, precision=highest)

    nest_ext = with_halo(nest_state, halo)
    is_south = (nest_global == -1)[None, :, None]
    is_north = (nest_global == nest_total)[None, :, None]

    def fix(field, f):
        return jnp.where(
            is_south,
            ends[:, f, 0][:, None, :],
            jnp.where(is_north, ends[:, f, 1][:, None, :], field),
        )

    def dx(field, f):
        west_col = side_ext[:, f, 0][:, :, None]
        east_col = side_ext[:, f, 1][:, :, None]
        right = jnp.concatenate([field[:, :, 1:], east_col], axis=2)
        left = jnp.concatenate([west_col, field[:, :, :-1]], axis=2)
        return 0.5 * (right - left)

    def dy(field):
        zero = jnp.zeros_like(field[:, :1])
        up = jnp.concatenate([field[:, 1:], zero], axis=1)
        down = jnp.concatenate([zero, field[:, :-1]], axis=1)
        return 0.5 * (up - down)

    height, zonal, meridional = (nest_ext[:, 0], nest_ext[:, 1], nest_ext[:, 2])
    for _ in range(NSTEPS):
        zonal_fixed = fix(zonal, 1)
        merid_fixed = fix(meridional, 2)
        height_new = height - courant * (dx(zonal_fixed, 1) + dy(merid_fixed))
        height_fixed = fix(height_new, 0)
        zonal_new = (1.0 - friction) * zonal - courant * dx(height_fixed, 0) + rotation * meridional
        merid_new = (1.0 - friction) * meridional - courant * dy(height_fixed) - rotation * zonal
        height, zonal, meridional = height_new, zonal_new, merid_new
    nest = jnp.stack([height, zonal, meridional], axis=1)[:, :, halo : halo + nest_rows]

    block_cols = (
        jnp.arange(nest_width, dtype=jnp.int32)[:, None] // 3
        == jnp.arange(span, dtype=jnp.int32)[None, :]
    ).astype(jnp.float32)
    col_sums = jnp.einsum("mfrj,jp->mfrp", nest, block_cols, precision=highest)
    coarse = col_sums.reshape(members, 3, tile_coarse, 3, span).sum(axis=3) / 9.0

    shift = (rows_off + tile_coarse - 1) // tile_coarse - 1
    moved = coarse
    reach = 1
    while reach < bands:
        count = min(4, bands // reach)
        digit = (shift // reach) % count
        chosen = moved
        for k in range(1, count):
            recv = lax.ppermute(moved, "band", [(i, (i + k * reach) % bands) for i in range(bands)])
            chosen = jnp.where((digit == k)[:, None, None, None], recv, chosen)
        moved = chosen
        reach *= count
    half = bands // 2
    low_half = band_index < half
    pieces = []
    for i in range(3):
        got = []
        for h in range(2):
            pairs = [((2 * p - 1 + i) % bands, p) for p in range(h * half, (h + 1) * half)]
            got.append(lax.ppermute(moved, "band", pairs))
        pieces.append(jnp.where(low_half, got[0], got[1]))
    near = jnp.concatenate(pieces, axis=2)
    lead = tile_coarse * (shift + 1) - rows_off
    patch = jax.vmap(lambda blk, e: lax.dynamic_slice_in_dim(blk, e, band_rows, axis=1))(near, lead)

    relative_rows = global_rows[None, :] - rows_off[:, None]
    covered = (relative_rows >= 0) & (relative_rows < span)
    parent_out = stepped
    for m in range(members):
        start = (m, 0, 0, cols_off[m])
        current = lax.dynamic_slice(parent_out, start, (1, 3, band_rows, span))
        merged = jnp.where(covered[m][None, None, :, None], patch[m : m + 1], current)
        parent_out = lax.dynamic_update_slice(parent_out, merged, start)
    return (parent_out, nest)


def solution(mesh):
    in_specs = (P("member", None, "band", None), P("member", None, "band", None), P("member", None))
    out_specs = (P("member", None, "band", None), P("member", None, "band", None))
    return jax.shard_map(
        per_device, mesh=mesh, in_specs=in_specs, out_specs=out_specs, check_vma=False
    )
```

```python
import jax
import jax.numpy as jnp
from jax import lax
from jax.sharding import PartitionSpec as P

NSTEPS = 3


courant = 0.9
friction = 0.02
rotation = 0.05
highest = lax.Precision.HIGHEST


def shift_pairs(count, shift):
    if shift > 0:
        return [(i, i + shift) for i in range(count - shift)]
    return [(i, i + shift) for i in range(-shift, count)]


def with_halo(cells, width):
    count = lax.axis_size("band")
    head = cells[:, :, :width]
    tail = cells[:, :, cells.shape[2] - width :]
    return jnp.concatenate(
        [
            lax.ppermute(tail, "band", shift_pairs(count, 1)),
            cells,
            lax.ppermute(head, "band", shift_pairs(count, -1)),
        ],
        axis=2,
    )


def interp_matrix(fine, coarse_count):
    rows = jnp.arange(fine, dtype=jnp.int32)[:, None] + 1
    cols = jnp.arange(coarse_count, dtype=jnp.int32)[None, :]
    base = rows // 3
    frac = rows % 3
    upper = frac.astype(jnp.float32) / 3.0
    lower = (3 - frac).astype(jnp.float32) / 3.0
    return jnp.where(cols == base, lower, 0.0) + jnp.where(cols == base + 1, upper, 0.0)


def shift_cols(field):
    return 0.5 * (jnp.roll(field, -1, axis=-1) - jnp.roll(field, 1, axis=-1))


def parent_step(parent_state):
    height, zonal, meridional = (parent_state[:, 0], parent_state[:, 1], parent_state[:, 2])
    merid_ext = with_halo(meridional[:, None], 1)[:, 0]
    height_new = height - courant * (
        shift_cols(zonal) + 0.5 * (merid_ext[:, 2:] - merid_ext[:, :-2])
    )
    height_ext = with_halo(height_new[:, None], 1)[:, 0]
    zonal_new = (1.0 - friction) * zonal - courant * shift_cols(height_new) + rotation * meridional
    merid_new = (
        (1.0 - friction) * meridional
        - courant * (0.5 * (height_ext[:, 2:] - height_ext[:, :-2]))
        - rotation * zonal
    )
    return jnp.stack([height_new, zonal_new, merid_new], axis=1)


def per_device(parent_state, nest_state, offsets):
    members = parent_state.shape[0]
    band_rows = parent_state.shape[2]
    nest_rows = nest_state.shape[2]
    nest_width = nest_state.shape[3]
    span = nest_width // 3
    tile_coarse = nest_rows // 3
    bands = lax.axis_size("band")
    band_index = lax.axis_index("band")
    parent_total = bands * band_rows
    nest_total = bands * nest_rows
    halo = 2 * NSTEPS
    ext_rows = nest_rows + 2 * halo
    rows_off = offsets[:, 0]
    cols_off = offsets[:, 1]
    two = jnp.float32(2.0) / jnp.float32(3.0)
    one = jnp.float32(1.0) / jnp.float32(3.0)

    stepped = parent_step(parent_state)

    colslice = jnp.concatenate(
        [
            lax.dynamic_slice(stepped, (m, 0, 0, cols_off[m] - 1), (1, 3, band_rows, span + 2))
            for m in range(members)
        ],
        axis=0,
    )

    window_cols = jnp.arange(span + 2, dtype=jnp.int32)[:, None]
    west_side = jnp.arange(2, dtype=jnp.int32)[None, :] == 0
    column_weights = (
        jnp.where(west_side & (window_cols == 0), two, 0.0)
        + jnp.where(west_side & (window_cols == 1), one, 0.0)
        + jnp.where(~west_side & (window_cols == span), one, 0.0)
        + jnp.where(~west_side & (window_cols == span + 1), two, 0.0)
    )
    strip = jnp.einsum("mflq,qs->mfsl", colslice, column_weights, precision=highest)
    strip = strip.reshape(members * 6, band_rows)

    global_rows = band_index * band_rows + jnp.arange(band_rows, dtype=jnp.int32)
    row_start = rows_off[:, None]
    south_weight = jnp.where(global_rows[None, :] == row_start - 1, two, 0.0) + jnp.where(
        global_rows[None, :] == row_start, one, 0.0
    )
    north_weight = jnp.where(global_rows[None, :] == row_start + span - 1, one, 0.0) + jnp.where(
        global_rows[None, :] == row_start + span, two, 0.0
    )
    row_weights = jnp.stack([south_weight, north_weight], axis=1)
    ends_part = jnp.einsum("msl,mflq->mfsq", row_weights, colslice, precision=highest)

    blocks = strip
    sums = ends_part.reshape(members * 6, span + 2)
    reach = 1
    while reach < bands:
        count = min(4, bands // reach)
        payload = jnp.concatenate([blocks, sums], axis=1)
        width = blocks.shape[1]
        recvs = [
            lax.ppermute(payload, "band", [(i, (i + k * reach) % bands) for i in range(bands)])
            for k in range(count - 1, 0, -1)
        ]
        blocks = jnp.concatenate([got[:, :width] for got in recvs] + [blocks], axis=1)
        for got in recvs:
            sums = sums + got[:, width:]
        reach *= count
    strip_all = blocks.reshape(members, 3, 2, parent_total)
    held_rows = ((band_index + 1) * band_rows + jnp.arange(parent_total, dtype=jnp.int32)) % parent_total
    ends_full = sums.reshape(members, 3, 2, span + 2)
    inner_weights = interp_matrix(nest_width + 2, span + 2)[1:-1]
    ends = jnp.einsum("jq,mfsq->mfsj", inner_weights, ends_full, precision=highest)

    nest_global = band_index * nest_rows - halo + jnp.arange(ext_rows, dtype=jnp.int32)
    base = (nest_global + 2) // 3
    frac = (nest_global + 2) % 3
    lower = (3 - frac).astype(jnp.float32) / 3.0
    upper = frac.astype(jnp.float32) / 3.0
    first_row = rows_off[:, None] - 1 + base[None, :]
    all_rows = held_rows[None, None, :]
    side_weights = jnp.where(all_rows == first_row[:, :, None], lower[None, :, None], 0.0) + jnp.where(
        all_rows == first_row[:, :, None] + 1, upper[None, :, None], 0.0
    )
    side_ext = jnp.einsum("mkr,mfsr->mfsk", side_weights, strip_all, precision=highest)

    nest_ext = with_halo(nest_state, halo)
    is_south = (nest_global == -1)[None, :, None]
    is_north = (nest_global == nest_total)[None, :, None]

    def fix(field, f):
        return jnp.where(
            is_south,
            ends[:, f, 0][:, None, :],
            jnp.where(is_north, ends[:, f, 1][:, None, :], field),
        )

    def dx(field, f):
        west_col = side_ext[:, f, 0][:, :, None]
        east_col = side_ext[:, f, 1][:, :, None]
        right = jnp.concatenate([field[:, :, 1:], east_col], axis=2)
        left = jnp.concatenate([west_col, field[:, :, :-1]], axis=2)
        return 0.5 * (right - left)

    def dy(field):
        zero = jnp.zeros_like(field[:, :1])
        up = jnp.concatenate([field[:, 1:], zero], axis=1)
        down = jnp.concatenate([zero, field[:, :-1]], axis=1)
        return 0.5 * (up - down)

    height, zonal, meridional = (nest_ext[:, 0], nest_ext[:, 1], nest_ext[:, 2])
    for _ in range(NSTEPS):
        zonal_fixed = fix(zonal, 1)
        merid_fixed = fix(meridional, 2)
        height_new = height - courant * (dx(zonal_fixed, 1) + dy(merid_fixed))
        height_fixed = fix(height_new, 0)
        zonal_new = (1.0 - friction) * zonal - courant * dx(height_fixed, 0) + rotation * meridional
        merid_new = (1.0 - friction) * meridional - courant * dy(height_fixed) - rotation * zonal
        height, zonal, meridional = height_new, zonal_new, merid_new
    nest = jnp.stack([height, zonal, meridional], axis=1)[:, :, halo : halo + nest_rows]

    block_cols = (
        jnp.arange(nest_width, dtype=jnp.int32)[:, None] // 3
        == jnp.arange(span, dtype=jnp.int32)[None, :]
    ).astype(jnp.float32)
    col_sums = jnp.einsum("mfrj,jp->mfrp", nest, block_cols, precision=highest)
    coarse = col_sums.reshape(members, 3, tile_coarse, 3, span).sum(axis=3) / 9.0

    shift = (rows_off + tile_coarse - 1) // tile_coarse - 1
    moved = coarse
    reach = 1
    while reach < bands:
        count = min(4, bands // reach)
        digit = (shift // reach) % count
        chosen = moved
        for k in range(1, count):
            recv = lax.ppermute(moved, "band", [(i, (i + k * reach) % bands) for i in range(bands)])
            chosen = jnp.where((digit == k)[:, None, None, None], recv, chosen)
        moved = chosen
        reach *= count
    half = bands // 2
    low_half = band_index < half
    pieces = []
    for i in range(3):
        got = []
        for h in range(2):
            pairs = [((2 * p - 1 + i) % bands, p) for p in range(h * half, (h + 1) * half)]
            got.append(lax.ppermute(moved, "band", pairs))
        pieces.append(jnp.where(low_half, got[0], got[1]))
    near = jnp.concatenate(pieces, axis=2)
    lead = tile_coarse * (shift + 1) - rows_off
    patch = jax.vmap(lambda blk, e: lax.dynamic_slice_in_dim(blk, e, band_rows, axis=1))(near, lead)

    relative_rows = global_rows[None, :] - rows_off[:, None]
    covered = (relative_rows >= 0) & (relative_rows < span)
    parent_out = stepped
    for m in range(members):
        start = (m, 0, 0, cols_off[m])
        current = lax.dynamic_slice(parent_out, start, (1, 3, band_rows, span))
        merged = jnp.where(covered[m][None, None, :, None], patch[m : m + 1], current)
        parent_out = lax.dynamic_update_slice(parent_out, merged, start)
    return (parent_out, nest)


def solution(mesh):
    in_specs = (P("member", None, "band", None), P("member", None, "band", None), P("member", None))
    out_specs = (P("member", None, "band", None), P("member", None, "band", None))
    return jax.shard_map(
        per_device, mesh=mesh, in_specs=in_specs, out_specs=out_specs, check_vma=False
    )
```

```python
import jax
import jax.numpy as jnp
from jax import lax
from jax.sharding import PartitionSpec as P

NSTEPS = 3


courant = 0.9
friction = 0.02
rotation = 0.05
highest = lax.Precision.HIGHEST


def shift_pairs(count, shift):
    if shift > 0:
        return [(i, i + shift) for i in range(count - shift)]
    return [(i, i + shift) for i in range(-shift, count)]


def with_halo(cells, width):
    count = lax.axis_size("band")
    head = cells[:, :, :width]
    tail = cells[:, :, cells.shape[2] - width :]
    return jnp.concatenate(
        [
            lax.ppermute(tail, "band", shift_pairs(count, 1)),
            cells,
            lax.ppermute(head, "band", shift_pairs(count, -1)),
        ],
        axis=2,
    )


def interp_matrix(fine, coarse_count):
    rows = jnp.arange(fine, dtype=jnp.int32)[:, None] + 1
    cols = jnp.arange(coarse_count, dtype=jnp.int32)[None, :]
    base = rows // 3
    frac = rows % 3
    upper = frac.astype(jnp.float32) / 3.0
    lower = (3 - frac).astype(jnp.float32) / 3.0
    return jnp.where(cols == base, lower, 0.0) + jnp.where(cols == base + 1, upper, 0.0)


def shift_cols(field):
    return 0.5 * (jnp.roll(field, -1, axis=-1) - jnp.roll(field, 1, axis=-1))


def parent_step(parent_state):
    height, zonal, meridional = (parent_state[:, 0], parent_state[:, 1], parent_state[:, 2])
    count = lax.axis_size("band")
    band_index = lax.axis_index("band")
    rows = height.shape[1]
    tail = jnp.stack(
        [meridional[:, rows - 2], meridional[:, rows - 1], zonal[:, rows - 1], height[:, rows - 1]], axis=1
    )
    head = jnp.stack([meridional[:, 0], meridional[:, 1], zonal[:, 0], height[:, 0]], axis=1)
    prev = lax.ppermute(tail, "band", shift_pairs(count, 1))
    next_ = lax.ppermute(head, "band", shift_pairs(count, -1))
    merid_ext = jnp.concatenate([prev[:, 1:2], meridional, next_[:, 0:1]], axis=1)
    height_new = height - courant * (
        shift_cols(zonal) + 0.5 * (merid_ext[:, 2:] - merid_ext[:, :-2])
    )
    height_prev = prev[:, 3] - courant * (
        shift_cols(prev[:, 2]) + 0.5 * (meridional[:, 0] - prev[:, 0])
    )
    height_next = next_[:, 3] - courant * (
        shift_cols(next_[:, 2]) + 0.5 * (next_[:, 1] - meridional[:, rows - 1])
    )
    height_prev = jnp.where(band_index == 0, 0.0, height_prev)
    height_next = jnp.where(band_index == count - 1, 0.0, height_next)
    height_ext = jnp.concatenate([height_prev[:, None], height_new, height_next[:, None]], axis=1)
    zonal_new = (1.0 - friction) * zonal - courant * shift_cols(height_new) + rotation * meridional
    merid_new = (
        (1.0 - friction) * meridional
        - courant * (0.5 * (height_ext[:, 2:] - height_ext[:, :-2]))
        - rotation * zonal
    )
    return jnp.stack([height_new, zonal_new, merid_new], axis=1)


def per_device(parent_state, nest_state, offsets):
    members = parent_state.shape[0]
    band_rows = parent_state.shape[2]
    nest_rows = nest_state.shape[2]
    nest_width = nest_state.shape[3]
    span = nest_width // 3
    tile_coarse = nest_rows // 3
    bands = lax.axis_size("band")
    band_index = lax.axis_index("band")
    parent_total = bands * band_rows
    nest_total = bands * nest_rows
    halo = 2 * NSTEPS
    ext_rows = nest_rows + 2 * halo
    rows_off = offsets[:, 0]
    cols_off = offsets[:, 1]
    two = jnp.float32(2.0) / jnp.float32(3.0)
    one = jnp.float32(1.0) / jnp.float32(3.0)

    stepped = parent_step(parent_state)

    colslice = jnp.concatenate(
        [
            lax.dynamic_slice(stepped, (m, 0, 0, cols_off[m] - 1), (1, 3, band_rows, span + 2))
            for m in range(members)
        ],
        axis=0,
    )

    window_cols = jnp.arange(span + 2, dtype=jnp.int32)[:, None]
    west_side = jnp.arange(2, dtype=jnp.int32)[None, :] == 0
    column_weights = (
        jnp.where(west_side & (window_cols == 0), two, 0.0)
        + jnp.where(west_side & (window_cols == 1), one, 0.0)
        + jnp.where(~west_side & (window_cols == span), one, 0.0)
        + jnp.where(~west_side & (window_cols == span + 1), two, 0.0)
    )
    strip = jnp.einsum("mflq,qs->mfsl", colslice, column_weights, precision=highest)
    strip = strip.reshape(members * 6, band_rows)

    global_rows = band_index * band_rows + jnp.arange(band_rows, dtype=jnp.int32)
    row_start = rows_off[:, None]
    south_weight = jnp.where(global_rows[None, :] == row_start - 1, two, 0.0) + jnp.where(
        global_rows[None, :] == row_start, one, 0.0
    )
    north_weight = jnp.where(global_rows[None, :] == row_start + span - 1, one, 0.0) + jnp.where(
        global_rows[None, :] == row_start + span, two, 0.0
    )
    row_weights = jnp.stack([south_weight, north_weight], axis=1)
    ends_part = jnp.einsum("msl,mflq->mfsq", row_weights, colslice, precision=highest)

    blocks = strip
    sums = ends_part.reshape(members * 6, span + 2)
    reach = 1
    while reach < bands:
        count = min(8, bands // reach)
        payload = jnp.concatenate([blocks, sums], axis=1)
        width = blocks.shape[1]
        recvs = [
            lax.ppermute(payload, "band", [(i, (i + k * reach) % bands) for i in range(bands)])
            for k in range(count - 1, 0, -1)
        ]
        blocks = jnp.concatenate([got[:, :width] for got in recvs] + [blocks], axis=1)
        for got in recvs:
            sums = sums + got[:, width:]
        reach *= count
    strip_all = blocks.reshape(members, 3, 2, parent_total)
    held_rows = ((band_index + 1) * band_rows + jnp.arange(parent_total, dtype=jnp.int32)) % parent_total
    ends_full = sums.reshape(members, 3, 2, span + 2)
    inner_weights = interp_matrix(nest_width + 2, span + 2)[1:-1]
    ends = jnp.einsum("jq,mfsq->mfsj", inner_weights, ends_full, precision=highest)

    nest_global = band_index * nest_rows - halo + jnp.arange(ext_rows, dtype=jnp.int32)
    base = (nest_global + 2) // 3
    frac = (nest_global + 2) % 3
    lower = (3 - frac).astype(jnp.float32) / 3.0
    upper = frac.astype(jnp.float32) / 3.0
    first_row = rows_off[:, None] - 1 + base[None, :]
    all_rows = held_rows[None, None, :]
    side_weights = jnp.where(all_rows == first_row[:, :, None], lower[None, :, None], 0.0) + jnp.where(
        all_rows == first_row[:, :, None] + 1, upper[None, :, None], 0.0
    )
    side_ext = jnp.einsum("mkr,mfsr->mfsk", side_weights, strip_all, precision=highest)

    nest_ext = with_halo(nest_state, halo)
    is_south = (nest_global == -1)[None, :, None]
    is_north = (nest_global == nest_total)[None, :, None]

    def fix(field, f):
        return jnp.where(
            is_south,
            ends[:, f, 0][:, None, :],
            jnp.where(is_north, ends[:, f, 1][:, None, :], field),
        )

    def dx(field, f):
        west_col = side_ext[:, f, 0][:, :, None]
        east_col = side_ext[:, f, 1][:, :, None]
        right = jnp.concatenate([field[:, :, 1:], east_col], axis=2)
        left = jnp.concatenate([west_col, field[:, :, :-1]], axis=2)
        return 0.5 * (right - left)

    def dy(field):
        zero = jnp.zeros_like(field[:, :1])
        up = jnp.concatenate([field[:, 1:], zero], axis=1)
        down = jnp.concatenate([zero, field[:, :-1]], axis=1)
        return 0.5 * (up - down)

    height, zonal, meridional = (nest_ext[:, 0], nest_ext[:, 1], nest_ext[:, 2])
    for _ in range(NSTEPS):
        zonal_fixed = fix(zonal, 1)
        merid_fixed = fix(meridional, 2)
        height_new = height - courant * (dx(zonal_fixed, 1) + dy(merid_fixed))
        height_fixed = fix(height_new, 0)
        zonal_new = (1.0 - friction) * zonal - courant * dx(height_fixed, 0) + rotation * meridional
        merid_new = (1.0 - friction) * meridional - courant * dy(height_fixed) - rotation * zonal
        height, zonal, meridional = height_new, zonal_new, merid_new
    nest = jnp.stack([height, zonal, meridional], axis=1)[:, :, halo : halo + nest_rows]

    block_cols = (
        jnp.arange(nest_width, dtype=jnp.int32)[:, None] // 3
        == jnp.arange(span, dtype=jnp.int32)[None, :]
    ).astype(jnp.float32)
    col_sums = jnp.einsum("mfrj,jp->mfrp", nest, block_cols, precision=highest)
    coarse = col_sums.reshape(members, 3, tile_coarse, 3, span).sum(axis=3) / 9.0

    radix = 4
    band_shift = rows_off // band_rows
    sub_shift = rows_off % band_rows
    low_digit = band_shift % radix
    high_digit = band_shift // radix
    lowest = -2 * (radix - 1) - 2
    fetched = []
    for k in range(lowest, 2):
        pairs = [(2 * p + k, p) for p in range(bands) if 0 <= 2 * p + k < bands]
        fetched.append(lax.ppermute(coarse, "band", pairs))
    stacked = jnp.concatenate(fetched, axis=2)
    lead = (-lowest) * tile_coarse - band_rows * low_digit - sub_shift
    near = jax.vmap(lambda blk, e: lax.dynamic_slice_in_dim(blk, e, band_rows, axis=1))(stacked, lead)
    patch = near
    for j in range(1, radix):
        recv = lax.ppermute(near, "band", shift_pairs(bands, j * radix))
        patch = jnp.where((high_digit == j)[:, None, None, None], recv, patch)

    relative_rows = global_rows[None, :] - rows_off[:, None]
    covered = (relative_rows >= 0) & (relative_rows < span)
    parent_out = stepped
    for m in range(members):
        start = (m, 0, 0, cols_off[m])
        current = lax.dynamic_slice(parent_out, start, (1, 3, band_rows, span))
        merged = jnp.where(covered[m][None, None, :, None], patch[m : m + 1], current)
        parent_out = lax.dynamic_update_slice(parent_out, merged, start)
    return (parent_out, nest)


def solution(mesh):
    in_specs = (P("member", None, "band", None), P("member", None, "band", None), P("member", None))
    out_specs = (P("member", None, "band", None), P("member", None, "band", None))
    return jax.shard_map(
        per_device, mesh=mesh, in_specs=in_specs, out_specs=out_specs, check_vma=False
    )
```

```python
import jax
import jax.numpy as jnp
from jax import lax
from jax.sharding import PartitionSpec as P

NSTEPS = 3


courant = 0.9
friction = 0.02
rotation = 0.05
highest = lax.Precision.HIGHEST


def shift_pairs(count, shift):
    if shift > 0:
        return [(i, i + shift) for i in range(count - shift)]
    return [(i, i + shift) for i in range(-shift, count)]


def with_halo(cells, width):
    count = lax.axis_size("band")
    head = cells[:, :, :width]
    tail = cells[:, :, cells.shape[2] - width :]
    return jnp.concatenate(
        [
            lax.ppermute(tail, "band", shift_pairs(count, 1)),
            cells,
            lax.ppermute(head, "band", shift_pairs(count, -1)),
        ],
        axis=2,
    )


def interp_matrix(fine, coarse_count):
    rows = jnp.arange(fine, dtype=jnp.int32)[:, None] + 1
    cols = jnp.arange(coarse_count, dtype=jnp.int32)[None, :]
    base = rows // 3
    frac = rows % 3
    upper = frac.astype(jnp.float32) / 3.0
    lower = (3 - frac).astype(jnp.float32) / 3.0
    return jnp.where(cols == base, lower, 0.0) + jnp.where(cols == base + 1, upper, 0.0)


def shift_cols(field):
    return 0.5 * (jnp.roll(field, -1, axis=-1) - jnp.roll(field, 1, axis=-1))


def parent_step(parent_state):
    height, zonal, meridional = (parent_state[:, 0], parent_state[:, 1], parent_state[:, 2])
    count = lax.axis_size("band")
    band_index = lax.axis_index("band")
    rows = height.shape[1]
    tail = jnp.stack(
        [meridional[:, rows - 2], meridional[:, rows - 1], zonal[:, rows - 1], height[:, rows - 1]], axis=1
    )
    head = jnp.stack([meridional[:, 0], meridional[:, 1], zonal[:, 0], height[:, 0]], axis=1)
    prev = lax.ppermute(tail, "band", shift_pairs(count, 1))
    next_ = lax.ppermute(head, "band", shift_pairs(count, -1))
    merid_ext = jnp.concatenate([prev[:, 1:2], meridional, next_[:, 0:1]], axis=1)
    height_new = height - courant * (
        shift_cols(zonal) + 0.5 * (merid_ext[:, 2:] - merid_ext[:, :-2])
    )
    height_prev = prev[:, 3] - courant * (
        shift_cols(prev[:, 2]) + 0.5 * (meridional[:, 0] - prev[:, 0])
    )
    height_next = next_[:, 3] - courant * (
        shift_cols(next_[:, 2]) + 0.5 * (next_[:, 1] - meridional[:, rows - 1])
    )
    height_prev = jnp.where(band_index == 0, 0.0, height_prev)
    height_next = jnp.where(band_index == count - 1, 0.0, height_next)
    height_ext = jnp.concatenate([height_prev[:, None], height_new, height_next[:, None]], axis=1)
    zonal_new = (1.0 - friction) * zonal - courant * shift_cols(height_new) + rotation * meridional
    merid_new = (
        (1.0 - friction) * meridional
        - courant * (0.5 * (height_ext[:, 2:] - height_ext[:, :-2]))
        - rotation * zonal
    )
    return jnp.stack([height_new, zonal_new, merid_new], axis=1)


def per_device(parent_state, nest_state, offsets):
    members = parent_state.shape[0]
    band_rows = parent_state.shape[2]
    nest_rows = nest_state.shape[2]
    nest_width = nest_state.shape[3]
    span = nest_width // 3
    tile_coarse = nest_rows // 3
    bands = lax.axis_size("band")
    band_index = lax.axis_index("band")
    parent_total = bands * band_rows
    nest_total = bands * nest_rows
    halo = 2 * NSTEPS
    ext_rows = nest_rows + 2 * halo
    rows_off = offsets[:, 0]
    cols_off = offsets[:, 1]
    two = jnp.float32(2.0) / jnp.float32(3.0)
    one = jnp.float32(1.0) / jnp.float32(3.0)

    stepped = parent_step(parent_state)

    colslice = jnp.concatenate(
        [
            lax.dynamic_slice(stepped, (m, 0, 0, cols_off[m] - 1), (1, 3, band_rows, span + 2))
            for m in range(members)
        ],
        axis=0,
    )

    window_cols = jnp.arange(span + 2, dtype=jnp.int32)[:, None]
    west_side = jnp.arange(2, dtype=jnp.int32)[None, :] == 0
    column_weights = (
        jnp.where(west_side & (window_cols == 0), two, 0.0)
        + jnp.where(west_side & (window_cols == 1), one, 0.0)
        + jnp.where(~west_side & (window_cols == span), one, 0.0)
        + jnp.where(~west_side & (window_cols == span + 1), two, 0.0)
    )
    strip = jnp.einsum("mflq,qs->mfsl", colslice, column_weights, precision=highest)
    strip = strip.reshape(members * 6, band_rows)

    global_rows = band_index * band_rows + jnp.arange(band_rows, dtype=jnp.int32)
    row_start = rows_off[:, None]
    south_weight = jnp.where(global_rows[None, :] == row_start - 1, two, 0.0) + jnp.where(
        global_rows[None, :] == row_start, one, 0.0
    )
    north_weight = jnp.where(global_rows[None, :] == row_start + span - 1, one, 0.0) + jnp.where(
        global_rows[None, :] == row_start + span, two, 0.0
    )
    row_weights = jnp.stack([south_weight, north_weight], axis=1)
    ends_part = jnp.einsum("msl,mflq->mfsq", row_weights, colslice, precision=highest)

    blocks = strip
    sums = ends_part.reshape(members * 6, span + 2)
    reach = 1
    while reach < bands:
        count = min(8, bands // reach)
        payload = jnp.concatenate([blocks, sums], axis=1)
        if reach == 1:
            nest_state, payload = lax.optimization_barrier((nest_state, payload))
        width = blocks.shape[1]
        recvs = [
            lax.ppermute(payload, "band", [(i, (i + k * reach) % bands) for i in range(bands)])
            for k in range(count - 1, 0, -1)
        ]
        blocks = jnp.concatenate([got[:, :width] for got in recvs] + [blocks], axis=1)
        for got in recvs:
            sums = sums + got[:, width:]
        reach *= count
    strip_all = blocks.reshape(members, 3, 2, parent_total)
    held_rows = ((band_index + 1) * band_rows + jnp.arange(parent_total, dtype=jnp.int32)) % parent_total
    ends_full = sums.reshape(members, 3, 2, span + 2)
    inner_weights = interp_matrix(nest_width + 2, span + 2)[1:-1]
    ends = jnp.einsum("jq,mfsq->mfsj", inner_weights, ends_full, precision=highest)

    nest_global = band_index * nest_rows - halo + jnp.arange(ext_rows, dtype=jnp.int32)
    base = (nest_global + 2) // 3
    frac = (nest_global + 2) % 3
    lower = (3 - frac).astype(jnp.float32) / 3.0
    upper = frac.astype(jnp.float32) / 3.0
    first_row = rows_off[:, None] - 1 + base[None, :]
    all_rows = held_rows[None, None, :]
    side_weights = jnp.where(all_rows == first_row[:, :, None], lower[None, :, None], 0.0) + jnp.where(
        all_rows == first_row[:, :, None] + 1, upper[None, :, None], 0.0
    )
    side_ext = jnp.einsum("mkr,mfsr->mfsk", side_weights, strip_all, precision=highest)

    nest_ext = with_halo(nest_state, halo)
    is_south = (nest_global == -1)[None, :, None]
    is_north = (nest_global == nest_total)[None, :, None]

    def fix(field, f):
        return jnp.where(
            is_south,
            ends[:, f, 0][:, None, :],
            jnp.where(is_north, ends[:, f, 1][:, None, :], field),
        )

    def dx(field, f):
        west_col = side_ext[:, f, 0][:, :, None]
        east_col = side_ext[:, f, 1][:, :, None]
        right = jnp.concatenate([field[:, :, 1:], east_col], axis=2)
        left = jnp.concatenate([west_col, field[:, :, :-1]], axis=2)
        return 0.5 * (right - left)

    def dy(field):
        zero = jnp.zeros_like(field[:, :1])
        up = jnp.concatenate([field[:, 1:], zero], axis=1)
        down = jnp.concatenate([zero, field[:, :-1]], axis=1)
        return 0.5 * (up - down)

    height, zonal, meridional = (nest_ext[:, 0], nest_ext[:, 1], nest_ext[:, 2])
    for _ in range(NSTEPS):
        zonal_fixed = fix(zonal, 1)
        merid_fixed = fix(meridional, 2)
        height_new = height - courant * (dx(zonal_fixed, 1) + dy(merid_fixed))
        height_fixed = fix(height_new, 0)
        zonal_new = (1.0 - friction) * zonal - courant * dx(height_fixed, 0) + rotation * meridional
        merid_new = (1.0 - friction) * meridional - courant * dy(height_fixed) - rotation * zonal
        height, zonal, meridional = height_new, zonal_new, merid_new
    nest = jnp.stack([height, zonal, meridional], axis=1)[:, :, halo : halo + nest_rows]

    block_cols = (
        jnp.arange(nest_width, dtype=jnp.int32)[:, None] // 3
        == jnp.arange(span, dtype=jnp.int32)[None, :]
    ).astype(jnp.float32)
    col_sums = jnp.einsum("mfrj,jp->mfrp", nest, block_cols, precision=highest)
    coarse = col_sums.reshape(members, 3, tile_coarse, 3, span).sum(axis=3) / 9.0

    radix = 4
    band_shift = rows_off // band_rows
    sub_shift = rows_off % band_rows
    low_digit = band_shift % radix
    high_digit = band_shift // radix
    lowest = -2 * (radix - 1) - 2
    fetched = []
    for k in range(lowest, 2):
        pairs = [(2 * p + k, p) for p in range(bands) if 0 <= 2 * p + k < bands]
        fetched.append(lax.ppermute(coarse, "band", pairs))
    stacked = jnp.concatenate(fetched, axis=2)
    lead = (-lowest) * tile_coarse - band_rows * low_digit - sub_shift
    near = jax.vmap(lambda blk, e: lax.dynamic_slice_in_dim(blk, e, band_rows, axis=1))(stacked, lead)
    patch = near
    for j in range(1, radix):
        recv = lax.ppermute(near, "band", shift_pairs(bands, j * radix))
        patch = jnp.where((high_digit == j)[:, None, None, None], recv, patch)

    relative_rows = global_rows[None, :] - rows_off[:, None]
    covered = (relative_rows >= 0) & (relative_rows < span)
    merged = jnp.where(covered[:, None, :, None], patch, colslice[..., 1 : span + 1])
    parent_out = stepped
    for m in range(members):
        parent_out = lax.dynamic_update_slice(parent_out, merged[m : m + 1], (m, 0, 0, cols_off[m]))
    return (parent_out, nest)


def solution(mesh):
    in_specs = (P("member", None, "band", None), P("member", None, "band", None), P("member", None))
    out_specs = (P("member", None, "band", None), P("member", None, "band", None))
    return jax.shard_map(
        per_device, mesh=mesh, in_specs=in_specs, out_specs=out_specs, check_vma=False
    )
```

```python
import jax
import jax.numpy as jnp
from jax import lax
from jax.sharding import PartitionSpec as P

NSTEPS = 3


courant = 0.9
friction = 0.02
rotation = 0.05
highest = lax.Precision.HIGHEST


def shift_pairs(count, shift):
    if shift > 0:
        return [(i, i + shift) for i in range(count - shift)]
    return [(i, i + shift) for i in range(-shift, count)]


def with_halo(cells, width):
    count = lax.axis_size("band")
    head = cells[:, :, :width]
    tail = cells[:, :, cells.shape[2] - width :]
    return jnp.concatenate(
        [
            lax.ppermute(tail, "band", shift_pairs(count, 1)),
            cells,
            lax.ppermute(head, "band", shift_pairs(count, -1)),
        ],
        axis=2,
    )


def interp_matrix(fine, coarse_count):
    rows = jnp.arange(fine, dtype=jnp.int32)[:, None] + 1
    cols = jnp.arange(coarse_count, dtype=jnp.int32)[None, :]
    base = rows // 3
    frac = rows % 3
    upper = frac.astype(jnp.float32) / 3.0
    lower = (3 - frac).astype(jnp.float32) / 3.0
    return jnp.where(cols == base, lower, 0.0) + jnp.where(cols == base + 1, upper, 0.0)


def shift_cols(field):
    return 0.5 * (jnp.roll(field, -1, axis=-1) - jnp.roll(field, 1, axis=-1))


def parent_step(parent_state):
    height, zonal, meridional = (parent_state[:, 0], parent_state[:, 1], parent_state[:, 2])
    count = lax.axis_size("band")
    band_index = lax.axis_index("band")
    rows = height.shape[1]
    tail = jnp.stack(
        [meridional[:, rows - 2], meridional[:, rows - 1], zonal[:, rows - 1], height[:, rows - 1]], axis=1
    )
    head = jnp.stack([meridional[:, 0], meridional[:, 1], zonal[:, 0], height[:, 0]], axis=1)
    prev = lax.ppermute(tail, "band", shift_pairs(count, 1))
    next_ = lax.ppermute(head, "band", shift_pairs(count, -1))
    merid_ext = jnp.concatenate([prev[:, 1:2], meridional, next_[:, 0:1]], axis=1)
    height_new = height - courant * (
        shift_cols(zonal) + 0.5 * (merid_ext[:, 2:] - merid_ext[:, :-2])
    )
    height_prev = prev[:, 3] - courant * (
        shift_cols(prev[:, 2]) + 0.5 * (meridional[:, 0] - prev[:, 0])
    )
    height_next = next_[:, 3] - courant * (
        shift_cols(next_[:, 2]) + 0.5 * (next_[:, 1] - meridional[:, rows - 1])
    )
    height_prev = jnp.where(band_index == 0, 0.0, height_prev)
    height_next = jnp.where(band_index == count - 1, 0.0, height_next)
    height_ext = jnp.concatenate([height_prev[:, None], height_new, height_next[:, None]], axis=1)
    zonal_new = (1.0 - friction) * zonal - courant * shift_cols(height_new) + rotation * meridional
    merid_new = (
        (1.0 - friction) * meridional
        - courant * (0.5 * (height_ext[:, 2:] - height_ext[:, :-2]))
        - rotation * zonal
    )
    return jnp.stack([height_new, zonal_new, merid_new], axis=1)


def per_device(parent_state, nest_state, offsets):
    members = parent_state.shape[0]
    band_rows = parent_state.shape[2]
    nest_rows = nest_state.shape[2]
    nest_width = nest_state.shape[3]
    span = nest_width // 3
    tile_coarse = nest_rows // 3
    bands = lax.axis_size("band")
    band_index = lax.axis_index("band")
    parent_total = bands * band_rows
    nest_total = bands * nest_rows
    halo = 2 * NSTEPS
    ext_rows = nest_rows + 2 * halo
    rows_off = offsets[:, 0]
    cols_off = offsets[:, 1]
    two = jnp.float32(2.0) / jnp.float32(3.0)
    one = jnp.float32(1.0) / jnp.float32(3.0)

    stepped = parent_step(parent_state)

    colslice = jnp.concatenate(
        [
            lax.dynamic_slice(stepped, (m, 0, 0, cols_off[m] - 1), (1, 3, band_rows, span + 2))
            for m in range(members)
        ],
        axis=0,
    )

    window_cols = jnp.arange(span + 2, dtype=jnp.int32)[:, None]
    west_side = jnp.arange(2, dtype=jnp.int32)[None, :] == 0
    column_weights = (
        jnp.where(west_side & (window_cols == 0), two, 0.0)
        + jnp.where(west_side & (window_cols == 1), one, 0.0)
        + jnp.where(~west_side & (window_cols == span), one, 0.0)
        + jnp.where(~west_side & (window_cols == span + 1), two, 0.0)
    )
    strip = jnp.einsum("mflq,qs->mfsl", colslice, column_weights, precision=highest)
    strip = strip.reshape(members * 6, band_rows)

    global_rows = band_index * band_rows + jnp.arange(band_rows, dtype=jnp.int32)
    row_start = rows_off[:, None]
    south_weight = jnp.where(global_rows[None, :] == row_start - 1, two, 0.0) + jnp.where(
        global_rows[None, :] == row_start, one, 0.0
    )
    north_weight = jnp.where(global_rows[None, :] == row_start + span - 1, one, 0.0) + jnp.where(
        global_rows[None, :] == row_start + span, two, 0.0
    )
    row_weights = jnp.stack([south_weight, north_weight], axis=1)
    ends_part = jnp.einsum("msl,mflq->mfsq", row_weights, colslice, precision=highest)

    blocks = strip
    sums = ends_part.reshape(members * 6, span + 2)
    reach = 1
    while reach < bands:
        count = min(8, bands // reach)
        payload = jnp.concatenate([blocks, sums], axis=1)
        if reach == 1:
            nest_state, payload = lax.optimization_barrier((nest_state, payload))
        width = blocks.shape[1]
        recvs = [
            lax.ppermute(payload, "band", [(i, (i + k * reach) % bands) for i in range(bands)])
            for k in range(count - 1, 0, -1)
        ]
        blocks = jnp.concatenate([got[:, :width] for got in recvs] + [blocks], axis=1)
        for got in recvs:
            sums = sums + got[:, width:]
        reach *= count
    strip_all = blocks.reshape(members, 3, 2, parent_total)
    held_rows = ((band_index + 1) * band_rows + jnp.arange(parent_total, dtype=jnp.int32)) % parent_total
    ends_full = sums.reshape(members, 3, 2, span + 2)
    inner_weights = interp_matrix(nest_width + 2, span + 2)[1:-1]
    ends = jnp.einsum("jq,mfsq->mfsj", inner_weights, ends_full, precision=highest)

    nest_global = band_index * nest_rows - halo + jnp.arange(ext_rows, dtype=jnp.int32)
    base = (nest_global + 2) // 3
    frac = (nest_global + 2) % 3
    lower = (3 - frac).astype(jnp.float32) / 3.0
    upper = frac.astype(jnp.float32) / 3.0
    first_row = rows_off[:, None] - 1 + base[None, :]
    all_rows = held_rows[None, None, :]
    side_weights = jnp.where(all_rows == first_row[:, :, None], lower[None, :, None], 0.0) + jnp.where(
        all_rows == first_row[:, :, None] + 1, upper[None, :, None], 0.0
    )
    side_ext = jnp.einsum("mkr,mfsr->mfsk", side_weights, strip_all, precision=highest)

    nest_ext = with_halo(nest_state, halo)
    is_south = (nest_global == -1)[None, :, None]
    is_north = (nest_global == nest_total)[None, :, None]

    def fix(field, f):
        return jnp.where(
            is_south,
            ends[:, f, 0][:, None, :],
            jnp.where(is_north, ends[:, f, 1][:, None, :], field),
        )

    def dx(field, f):
        west_col = side_ext[:, f, 0][:, :, None]
        east_col = side_ext[:, f, 1][:, :, None]
        right = jnp.concatenate([field[:, :, 1:], east_col], axis=2)
        left = jnp.concatenate([west_col, field[:, :, :-1]], axis=2)
        return 0.5 * (right - left)

    def dy(field):
        zero = jnp.zeros_like(field[:, :1])
        up = jnp.concatenate([field[:, 1:], zero], axis=1)
        down = jnp.concatenate([zero, field[:, :-1]], axis=1)
        return 0.5 * (up - down)

    height, zonal, meridional = (nest_ext[:, 0], nest_ext[:, 1], nest_ext[:, 2])
    for _ in range(NSTEPS):
        zonal_fixed = fix(zonal, 1)
        merid_fixed = fix(meridional, 2)
        height_new = height - courant * (dx(zonal_fixed, 1) + dy(merid_fixed))
        height_fixed = fix(height_new, 0)
        zonal_new = (1.0 - friction) * zonal - courant * dx(height_fixed, 0) + rotation * meridional
        merid_new = (1.0 - friction) * meridional - courant * dy(height_fixed) - rotation * zonal
        height, zonal, meridional = height_new, zonal_new, merid_new
    nest = jnp.stack([height, zonal, meridional], axis=1)[:, :, halo : halo + nest_rows]

    block_cols = (
        jnp.arange(nest_width, dtype=jnp.int32)[:, None] // 3
        == jnp.arange(span, dtype=jnp.int32)[None, :]
    ).astype(jnp.float32)
    col_sums = jnp.einsum("mfrj,jp->mfrp", nest, block_cols, precision=highest)
    coarse = col_sums.reshape(members, 3, tile_coarse, 3, span).sum(axis=3) / 9.0

    shift = (rows_off + tile_coarse - 1) // tile_coarse - 1
    moved = coarse
    step = 1
    while step < bands:
        recv = lax.ppermute(moved, "band", [(i, (i + step) % bands) for i in range(bands)])
        take = ((shift // step) % 2 == 1)[:, None, None, None]
        moved = jnp.where(take, recv, moved)
        step *= 2
    half = bands // 2
    low_half = band_index < half
    pieces = []
    for i in range(3):
        got = []
        for h in range(2):
            pairs = [((2 * p - 1 + i) % bands, p) for p in range(h * half, (h + 1) * half)]
            got.append(lax.ppermute(moved, "band", pairs))
        pieces.append(jnp.where(low_half, got[0], got[1]))
    near = jnp.concatenate(pieces, axis=2)
    lead = tile_coarse * (shift + 1) - rows_off
    patch = jax.vmap(lambda blk, e: lax.dynamic_slice_in_dim(blk, e, band_rows, axis=1))(near, lead)

    relative_rows = global_rows[None, :] - rows_off[:, None]
    covered = (relative_rows >= 0) & (relative_rows < span)
    merged = jnp.where(covered[:, None, :, None], patch, colslice[..., 1 : span + 1])
    parent_out = stepped
    for m in range(members):
        parent_out = lax.dynamic_update_slice(parent_out, merged[m : m + 1], (m, 0, 0, cols_off[m]))
    return (parent_out, nest)


def solution(mesh):
    in_specs = (P("member", None, "band", None), P("member", None, "band", None), P("member", None))
    out_specs = (P("member", None, "band", None), P("member", None, "band", None))
    return jax.shard_map(
        per_device, mesh=mesh, in_specs=in_specs, out_specs=out_specs, check_vma=False
    )
```

```python
import jax
import jax.numpy as jnp
from jax import lax
from jax.sharding import PartitionSpec as P

NSTEPS = 3


courant = 0.9
friction = 0.02
rotation = 0.05
highest = lax.Precision.HIGHEST


def shift_pairs(count, shift):
    if shift > 0:
        return [(i, i + shift) for i in range(count - shift)]
    return [(i, i + shift) for i in range(-shift, count)]


def with_halo(cells, width):
    count = lax.axis_size("band")
    head = cells[:, :, :width]
    tail = cells[:, :, cells.shape[2] - width :]
    return jnp.concatenate(
        [
            lax.ppermute(tail, "band", shift_pairs(count, 1)),
            cells,
            lax.ppermute(head, "band", shift_pairs(count, -1)),
        ],
        axis=2,
    )


def interp_matrix(fine, coarse_count):
    rows = jnp.arange(fine, dtype=jnp.int32)[:, None] + 1
    cols = jnp.arange(coarse_count, dtype=jnp.int32)[None, :]
    base = rows // 3
    frac = rows % 3
    upper = frac.astype(jnp.float32) / 3.0
    lower = (3 - frac).astype(jnp.float32) / 3.0
    return jnp.where(cols == base, lower, 0.0) + jnp.where(cols == base + 1, upper, 0.0)


def shift_cols(field):
    return 0.5 * (jnp.roll(field, -1, axis=-1) - jnp.roll(field, 1, axis=-1))


def parent_step(parent_state):
    height, zonal, meridional = (parent_state[:, 0], parent_state[:, 1], parent_state[:, 2])
    count = lax.axis_size("band")
    band_index = lax.axis_index("band")
    rows = height.shape[1]
    tail = jnp.stack(
        [meridional[:, rows - 2], meridional[:, rows - 1], zonal[:, rows - 1], height[:, rows - 1]], axis=1
    )
    head = jnp.stack([meridional[:, 0], meridional[:, 1], zonal[:, 0], height[:, 0]], axis=1)
    prev = lax.ppermute(tail, "band", shift_pairs(count, 1))
    next_ = lax.ppermute(head, "band", shift_pairs(count, -1))
    merid_ext = jnp.concatenate([prev[:, 1:2], meridional, next_[:, 0:1]], axis=1)
    height_new = height - courant * (
        shift_cols(zonal) + 0.5 * (merid_ext[:, 2:] - merid_ext[:, :-2])
    )
    height_prev = prev[:, 3] - courant * (
        shift_cols(prev[:, 2]) + 0.5 * (meridional[:, 0] - prev[:, 0])
    )
    height_next = next_[:, 3] - courant * (
        shift_cols(next_[:, 2]) + 0.5 * (next_[:, 1] - meridional[:, rows - 1])
    )
    height_prev = jnp.where(band_index == 0, 0.0, height_prev)
    height_next = jnp.where(band_index == count - 1, 0.0, height_next)
    height_ext = jnp.concatenate([height_prev[:, None], height_new, height_next[:, None]], axis=1)
    zonal_new = (1.0 - friction) * zonal - courant * shift_cols(height_new) + rotation * meridional
    merid_new = (
        (1.0 - friction) * meridional
        - courant * (0.5 * (height_ext[:, 2:] - height_ext[:, :-2]))
        - rotation * zonal
    )
    return jnp.stack([height_new, zonal_new, merid_new], axis=1), prev


def per_device(parent_state, nest_state, offsets):
    members = parent_state.shape[0]
    band_rows = parent_state.shape[2]
    nest_rows = nest_state.shape[2]
    nest_width = nest_state.shape[3]
    span = nest_width // 3
    tile_coarse = nest_rows // 3
    bands = lax.axis_size("band")
    band_index = lax.axis_index("band")
    parent_total = bands * band_rows
    nest_total = bands * nest_rows
    halo = 2 * NSTEPS
    ext_rows = nest_rows + 2 * halo
    rows_off = offsets[:, 0]
    cols_off = offsets[:, 1]
    two = jnp.float32(2.0) / jnp.float32(3.0)
    one = jnp.float32(1.0) / jnp.float32(3.0)

    stepped, arrived = parent_step(parent_state)
    nest_state, arrived = lax.optimization_barrier((nest_state, arrived))
    nest_ext = with_halo(nest_state, 2 * NSTEPS)

    colslice = jnp.concatenate(
        [
            lax.dynamic_slice(stepped, (m, 0, 0, cols_off[m] - 1), (1, 3, band_rows, span + 2))
            for m in range(members)
        ],
        axis=0,
    )

    window_cols = jnp.arange(span + 2, dtype=jnp.int32)[:, None]
    west_side = jnp.arange(2, dtype=jnp.int32)[None, :] == 0
    column_weights = (
        jnp.where(west_side & (window_cols == 0), two, 0.0)
        + jnp.where(west_side & (window_cols == 1), one, 0.0)
        + jnp.where(~west_side & (window_cols == span), one, 0.0)
        + jnp.where(~west_side & (window_cols == span + 1), two, 0.0)
    )
    strip = jnp.einsum("mflq,qs->mfsl", colslice, column_weights, precision=highest)
    strip = strip.reshape(members * 6, band_rows)

    global_rows = band_index * band_rows + jnp.arange(band_rows, dtype=jnp.int32)
    row_start = rows_off[:, None]
    south_weight = jnp.where(global_rows[None, :] == row_start - 1, two, 0.0) + jnp.where(
        global_rows[None, :] == row_start, one, 0.0
    )
    north_weight = jnp.where(global_rows[None, :] == row_start + span - 1, one, 0.0) + jnp.where(
        global_rows[None, :] == row_start + span, two, 0.0
    )
    row_weights = jnp.stack([south_weight, north_weight], axis=1)
    ends_part = jnp.einsum("msl,mflq->mfsq", row_weights, colslice, precision=highest)

    blocks = strip
    sums = ends_part.reshape(members * 6, span + 2)
    reach = 1
    while reach < bands:
        count = min(8, bands // reach)
        payload = jnp.concatenate([blocks, sums], axis=1)
        if reach == 1:
            payload, nest_ext = lax.optimization_barrier((payload, nest_ext))
        width = blocks.shape[1]
        recvs = [
            lax.ppermute(payload, "band", [(i, (i + k * reach) % bands) for i in range(bands)])
            for k in range(count - 1, 0, -1)
        ]
        blocks = jnp.concatenate([got[:, :width] for got in recvs] + [blocks], axis=1)
        for got in recvs:
            sums = sums + got[:, width:]
        reach *= count
    strip_all = blocks.reshape(members, 3, 2, parent_total)
    held_rows = ((band_index + 1) * band_rows + jnp.arange(parent_total, dtype=jnp.int32)) % parent_total
    ends_full = sums.reshape(members, 3, 2, span + 2)
    inner_weights = interp_matrix(nest_width + 2, span + 2)[1:-1]
    ends = jnp.einsum("jq,mfsq->mfsj", inner_weights, ends_full, precision=highest)

    nest_global = band_index * nest_rows - halo + jnp.arange(ext_rows, dtype=jnp.int32)
    base = (nest_global + 2) // 3
    frac = (nest_global + 2) % 3
    lower = (3 - frac).astype(jnp.float32) / 3.0
    upper = frac.astype(jnp.float32) / 3.0
    first_row = rows_off[:, None] - 1 + base[None, :]
    all_rows = held_rows[None, None, :]
    side_weights = jnp.where(all_rows == first_row[:, :, None], lower[None, :, None], 0.0) + jnp.where(
        all_rows == first_row[:, :, None] + 1, upper[None, :, None], 0.0
    )
    side_ext = jnp.einsum("mkr,mfsr->mfsk", side_weights, strip_all, precision=highest)

    is_south = (nest_global == -1)[None, :, None]
    is_north = (nest_global == nest_total)[None, :, None]

    def fix(field, f):
        return jnp.where(
            is_south,
            ends[:, f, 0][:, None, :],
            jnp.where(is_north, ends[:, f, 1][:, None, :], field),
        )

    def dx(field, f):
        west_col = side_ext[:, f, 0][:, :, None]
        east_col = side_ext[:, f, 1][:, :, None]
        right = jnp.concatenate([field[:, :, 1:], east_col], axis=2)
        left = jnp.concatenate([west_col, field[:, :, :-1]], axis=2)
        return 0.5 * (right - left)

    def dy(field):
        zero = jnp.zeros_like(field[:, :1])
        up = jnp.concatenate([field[:, 1:], zero], axis=1)
        down = jnp.concatenate([zero, field[:, :-1]], axis=1)
        return 0.5 * (up - down)

    height, zonal, meridional = (nest_ext[:, 0], nest_ext[:, 1], nest_ext[:, 2])
    for _ in range(NSTEPS):
        zonal_fixed = fix(zonal, 1)
        merid_fixed = fix(meridional, 2)
        height_new = height - courant * (dx(zonal_fixed, 1) + dy(merid_fixed))
        height_fixed = fix(height_new, 0)
        zonal_new = (1.0 - friction) * zonal - courant * dx(height_fixed, 0) + rotation * meridional
        merid_new = (1.0 - friction) * meridional - courant * dy(height_fixed) - rotation * zonal
        height, zonal, meridional = height_new, zonal_new, merid_new
    nest = jnp.stack([height, zonal, meridional], axis=1)[:, :, halo : halo + nest_rows]

    block_cols = (
        jnp.arange(nest_width, dtype=jnp.int32)[:, None] // 3
        == jnp.arange(span, dtype=jnp.int32)[None, :]
    ).astype(jnp.float32)
    col_sums = jnp.einsum("mfrj,jp->mfrp", nest, block_cols, precision=highest)
    coarse = col_sums.reshape(members, 3, tile_coarse, 3, span).sum(axis=3) / 9.0

    shift = (rows_off + tile_coarse - 1) // tile_coarse - 1
    moved = coarse
    step = 1
    while step < bands:
        recv = lax.ppermute(moved, "band", [(i, (i + step) % bands) for i in range(bands)])
        take = ((shift // step) % 2 == 1)[:, None, None, None]
        moved = jnp.where(take, recv, moved)
        step *= 2
    half = bands // 2
    low_half = band_index < half
    pieces = []
    for i in range(3):
        got = []
        for h in range(2):
            pairs = [((2 * p - 1 + i) % bands, p) for p in range(h * half, (h + 1) * half)]
            got.append(lax.ppermute(moved, "band", pairs))
        pieces.append(jnp.where(low_half, got[0], got[1]))
    near = jnp.concatenate(pieces, axis=2)
    lead = tile_coarse * (shift + 1) - rows_off
    patch = jax.vmap(lambda blk, e: lax.dynamic_slice_in_dim(blk, e, band_rows, axis=1))(near, lead)

    relative_rows = global_rows[None, :] - rows_off[:, None]
    covered = (relative_rows >= 0) & (relative_rows < span)
    merged = jnp.where(covered[:, None, :, None], patch, colslice[..., 1 : span + 1])
    parent_out = stepped
    for m in range(members):
        parent_out = lax.dynamic_update_slice(parent_out, merged[m : m + 1], (m, 0, 0, cols_off[m]))
    return (parent_out, nest)


def solution(mesh):
    in_specs = (P("member", None, "band", None), P("member", None, "band", None), P("member", None))
    out_specs = (P("member", None, "band", None), P("member", None, "band", None))
    return jax.shard_map(
        per_device, mesh=mesh, in_specs=in_specs, out_specs=out_specs, check_vma=False
    )
```

```python
import jax
import jax.numpy as jnp
from jax import lax
from jax.sharding import PartitionSpec as P

NSTEPS = 3


courant = 0.9
friction = 0.02
rotation = 0.05
highest = lax.Precision.HIGHEST


def shift_pairs(count, shift):
    if shift > 0:
        return [(i, i + shift) for i in range(count - shift)]
    return [(i, i + shift) for i in range(-shift, count)]


def with_halo(cells, width):
    count = lax.axis_size("band")
    head = cells[:, :, :width]
    tail = cells[:, :, cells.shape[2] - width :]
    return jnp.concatenate(
        [
            lax.ppermute(tail, "band", shift_pairs(count, 1)),
            cells,
            lax.ppermute(head, "band", shift_pairs(count, -1)),
        ],
        axis=2,
    )


def interp_matrix(fine, coarse_count):
    rows = jnp.arange(fine, dtype=jnp.int32)[:, None] + 1
    cols = jnp.arange(coarse_count, dtype=jnp.int32)[None, :]
    base = rows // 3
    frac = rows % 3
    upper = frac.astype(jnp.float32) / 3.0
    lower = (3 - frac).astype(jnp.float32) / 3.0
    return jnp.where(cols == base, lower, 0.0) + jnp.where(cols == base + 1, upper, 0.0)


def shift_cols(field):
    return 0.5 * (jnp.roll(field, -1, axis=-1) - jnp.roll(field, 1, axis=-1))


def parent_step(parent_state):
    height, zonal, meridional = (parent_state[:, 0], parent_state[:, 1], parent_state[:, 2])
    count = lax.axis_size("band")
    band_index = lax.axis_index("band")
    rows = height.shape[1]
    tail = jnp.stack(
        [meridional[:, rows - 2], meridional[:, rows - 1], zonal[:, rows - 1], height[:, rows - 1]], axis=1
    )
    head = jnp.stack([meridional[:, 0], meridional[:, 1], zonal[:, 0], height[:, 0]], axis=1)
    prev = lax.ppermute(tail, "band", shift_pairs(count, 1))
    next_ = lax.ppermute(head, "band", shift_pairs(count, -1))
    merid_ext = jnp.concatenate([prev[:, 1:2], meridional, next_[:, 0:1]], axis=1)
    height_new = height - courant * (
        shift_cols(zonal) + 0.5 * (merid_ext[:, 2:] - merid_ext[:, :-2])
    )
    height_prev = prev[:, 3] - courant * (
        shift_cols(prev[:, 2]) + 0.5 * (meridional[:, 0] - prev[:, 0])
    )
    height_next = next_[:, 3] - courant * (
        shift_cols(next_[:, 2]) + 0.5 * (next_[:, 1] - meridional[:, rows - 1])
    )
    height_prev = jnp.where(band_index == 0, 0.0, height_prev)
    height_next = jnp.where(band_index == count - 1, 0.0, height_next)
    height_ext = jnp.concatenate([height_prev[:, None], height_new, height_next[:, None]], axis=1)
    zonal_new = (1.0 - friction) * zonal - courant * shift_cols(height_new) + rotation * meridional
    merid_new = (
        (1.0 - friction) * meridional
        - courant * (0.5 * (height_ext[:, 2:] - height_ext[:, :-2]))
        - rotation * zonal
    )
    return jnp.stack([height_new, zonal_new, merid_new], axis=1)


def per_device(parent_state, nest_state, offsets):
    members = parent_state.shape[0]
    band_rows = parent_state.shape[2]
    nest_rows = nest_state.shape[2]
    nest_width = nest_state.shape[3]
    span = nest_width // 3
    tile_coarse = nest_rows // 3
    bands = lax.axis_size("band")
    band_index = lax.axis_index("band")
    parent_total = bands * band_rows
    nest_total = bands * nest_rows
    halo = 2 * NSTEPS
    ext_rows = nest_rows + 2 * halo
    rows_off = offsets[:, 0]
    cols_off = offsets[:, 1]
    two = jnp.float32(2.0) / jnp.float32(3.0)
    one = jnp.float32(1.0) / jnp.float32(3.0)

    stepped = parent_step(parent_state)

    colslice = jnp.concatenate(
        [
            lax.dynamic_slice(stepped, (m, 0, 0, cols_off[m] - 1), (1, 3, band_rows, span + 2))
            for m in range(members)
        ],
        axis=0,
    )

    window_cols = jnp.arange(span + 2, dtype=jnp.int32)[:, None]
    west_side = jnp.arange(2, dtype=jnp.int32)[None, :] == 0
    column_weights = (
        jnp.where(west_side & (window_cols == 0), two, 0.0)
        + jnp.where(west_side & (window_cols == 1), one, 0.0)
        + jnp.where(~west_side & (window_cols == span), one, 0.0)
        + jnp.where(~west_side & (window_cols == span + 1), two, 0.0)
    )
    strip = jnp.einsum("mflq,qs->mfsl", colslice, column_weights, precision=highest)
    strip = strip.reshape(members * 6, band_rows)

    global_rows = band_index * band_rows + jnp.arange(band_rows, dtype=jnp.int32)
    row_start = rows_off[:, None]
    south_weight = jnp.where(global_rows[None, :] == row_start - 1, two, 0.0) + jnp.where(
        global_rows[None, :] == row_start, one, 0.0
    )
    north_weight = jnp.where(global_rows[None, :] == row_start + span - 1, one, 0.0) + jnp.where(
        global_rows[None, :] == row_start + span, two, 0.0
    )
    row_weights = jnp.stack([south_weight, north_weight], axis=1)
    ends_part = jnp.einsum("msl,mflq->mfsq", row_weights, colslice, precision=highest)

    blocks = strip
    sums = ends_part.reshape(members * 6, span + 2)
    reach = 1
    while reach < bands:
        count = min(8, bands // reach)
        payload = jnp.concatenate([blocks, sums], axis=1)
        width = blocks.shape[1]
        recvs = [
            lax.ppermute(payload, "band", [(i, (i + k * reach) % bands) for i in range(bands)])
            for k in range(count - 1, 0, -1)
        ]
        blocks = jnp.concatenate([got[:, :width] for got in recvs] + [blocks], axis=1)
        for got in recvs:
            sums = sums + got[:, width:]
        reach *= count
    strip_all = blocks.reshape(members, 3, 2, parent_total)
    held_rows = ((band_index + 1) * band_rows + jnp.arange(parent_total, dtype=jnp.int32)) % parent_total
    ends_full = sums.reshape(members, 3, 2, span + 2)
    inner_weights = interp_matrix(nest_width + 2, span + 2)[1:-1]
    ends = jnp.einsum("jq,mfsq->mfsj", inner_weights, ends_full, precision=highest)

    nest_global = band_index * nest_rows - halo + jnp.arange(ext_rows, dtype=jnp.int32)
    base = (nest_global + 2) // 3
    frac = (nest_global + 2) % 3
    lower = (3 - frac).astype(jnp.float32) / 3.0
    upper = frac.astype(jnp.float32) / 3.0
    first_row = rows_off[:, None] - 1 + base[None, :]
    all_rows = held_rows[None, None, :]
    side_weights = jnp.where(all_rows == first_row[:, :, None], lower[None, :, None], 0.0) + jnp.where(
        all_rows == first_row[:, :, None] + 1, upper[None, :, None], 0.0
    )
    side_ext = jnp.einsum("mkr,mfsr->mfsk", side_weights, strip_all, precision=highest)

    nest_ext = with_halo(nest_state, halo)
    is_south = (nest_global == -1)[None, :, None]
    is_north = (nest_global == nest_total)[None, :, None]

    def fix(field, f):
        return jnp.where(
            is_south,
            ends[:, f, 0][:, None, :],
            jnp.where(is_north, ends[:, f, 1][:, None, :], field),
        )

    def dx(field, f):
        west_col = side_ext[:, f, 0][:, :, None]
        east_col = side_ext[:, f, 1][:, :, None]
        right = jnp.concatenate([field[:, :, 1:], east_col], axis=2)
        left = jnp.concatenate([west_col, field[:, :, :-1]], axis=2)
        return 0.5 * (right - left)

    def dy(field):
        zero = jnp.zeros_like(field[:, :1])
        up = jnp.concatenate([field[:, 1:], zero], axis=1)
        down = jnp.concatenate([zero, field[:, :-1]], axis=1)
        return 0.5 * (up - down)

    height, zonal, meridional = (nest_ext[:, 0], nest_ext[:, 1], nest_ext[:, 2])
    for _ in range(NSTEPS):
        zonal_fixed = fix(zonal, 1)
        merid_fixed = fix(meridional, 2)
        height_new = height - courant * (dx(zonal_fixed, 1) + dy(merid_fixed))
        height_fixed = fix(height_new, 0)
        zonal_new = (1.0 - friction) * zonal - courant * dx(height_fixed, 0) + rotation * meridional
        merid_new = (1.0 - friction) * meridional - courant * dy(height_fixed) - rotation * zonal
        height, zonal, meridional = height_new, zonal_new, merid_new
    nest = jnp.stack([height, zonal, meridional], axis=1)[:, :, halo : halo + nest_rows]

    block_cols = (
        jnp.arange(nest_width, dtype=jnp.int32)[:, None] // 3
        == jnp.arange(span, dtype=jnp.int32)[None, :]
    ).astype(jnp.float32)
    col_sums = jnp.einsum("mfrj,jp->mfrp", nest, block_cols, precision=highest)
    coarse = col_sums.reshape(members, 3, tile_coarse, 3, span).sum(axis=3) / 9.0

    shift = (rows_off + tile_coarse - 1) // tile_coarse - 1
    moved = coarse
    step = 1
    while step < bands:
        recv = lax.ppermute(moved, "band", [(i, (i + step) % bands) for i in range(bands)])
        take = ((shift // step) % 2 == 1)[:, None, None, None]
        moved = jnp.where(take, recv, moved)
        step *= 2
    half = bands // 2
    low_half = band_index < half
    pieces = []
    for i in range(3):
        got = []
        for h in range(2):
            pairs = [((2 * p - 1 + i) % bands, p) for p in range(h * half, (h + 1) * half)]
            got.append(lax.ppermute(moved, "band", pairs))
        pieces.append(jnp.where(low_half, got[0], got[1]))
    near = jnp.concatenate(pieces, axis=2)
    lead = tile_coarse * (shift + 1) - rows_off
    patch = jax.vmap(lambda blk, e: lax.dynamic_slice_in_dim(blk, e, band_rows, axis=1))(near, lead)

    relative_rows = global_rows[None, :] - rows_off[:, None]
    covered = (relative_rows >= 0) & (relative_rows < span)
    merged = jnp.where(covered[:, None, :, None], patch, colslice[..., 1 : span + 1])
    parent_out = stepped
    for m in range(members):
        parent_out = lax.dynamic_update_slice(parent_out, merged[m : m + 1], (m, 0, 0, cols_off[m]))
    return (parent_out, nest)


def solution(mesh):
    in_specs = (P("member", None, "band", None), P("member", None, "band", None), P("member", None))
    out_specs = (P("member", None, "band", None), P("member", None, "band", None))
    return jax.shard_map(
        per_device, mesh=mesh, in_specs=in_specs, out_specs=out_specs, check_vma=False
    )
```

```python
import jax
import jax.numpy as jnp
from jax import lax
from jax.sharding import PartitionSpec as P

NSTEPS = 3


courant = 0.9
friction = 0.02
rotation = 0.05
highest = lax.Precision.HIGHEST


def shift_pairs(count, shift):
    if shift > 0:
        return [(i, i + shift) for i in range(count - shift)]
    return [(i, i + shift) for i in range(-shift, count)]


def with_halo(cells, width):
    count = lax.axis_size("band")
    head = cells[:, :, :width]
    tail = cells[:, :, cells.shape[2] - width :]
    return jnp.concatenate(
        [
            lax.ppermute(tail, "band", shift_pairs(count, 1)),
            cells,
            lax.ppermute(head, "band", shift_pairs(count, -1)),
        ],
        axis=2,
    )


def interp_matrix(fine, coarse_count):
    rows = jnp.arange(fine, dtype=jnp.int32)[:, None] + 1
    cols = jnp.arange(coarse_count, dtype=jnp.int32)[None, :]
    base = rows // 3
    frac = rows % 3
    upper = frac.astype(jnp.float32) / 3.0
    lower = (3 - frac).astype(jnp.float32) / 3.0
    return jnp.where(cols == base, lower, 0.0) + jnp.where(cols == base + 1, upper, 0.0)


def shift_cols(field):
    return 0.5 * (jnp.roll(field, -1, axis=-1) - jnp.roll(field, 1, axis=-1))


def parent_step(parent_state):
    height, zonal, meridional = (parent_state[:, 0], parent_state[:, 1], parent_state[:, 2])
    count = lax.axis_size("band")
    band_index = lax.axis_index("band")
    rows = height.shape[1]
    tail = jnp.stack(
        [meridional[:, rows - 2], meridional[:, rows - 1], zonal[:, rows - 1], height[:, rows - 1]], axis=1
    )
    head = jnp.stack([meridional[:, 0], meridional[:, 1], zonal[:, 0], height[:, 0]], axis=1)
    prev = lax.ppermute(tail, "band", shift_pairs(count, 1))
    next_ = lax.ppermute(head, "band", shift_pairs(count, -1))
    merid_ext = jnp.concatenate([prev[:, 1:2], meridional, next_[:, 0:1]], axis=1)
    height_new = height - courant * (
        shift_cols(zonal) + 0.5 * (merid_ext[:, 2:] - merid_ext[:, :-2])
    )
    height_prev = prev[:, 3] - courant * (
        shift_cols(prev[:, 2]) + 0.5 * (meridional[:, 0] - prev[:, 0])
    )
    height_next = next_[:, 3] - courant * (
        shift_cols(next_[:, 2]) + 0.5 * (next_[:, 1] - meridional[:, rows - 1])
    )
    height_prev = jnp.where(band_index == 0, 0.0, height_prev)
    height_next = jnp.where(band_index == count - 1, 0.0, height_next)
    height_ext = jnp.concatenate([height_prev[:, None], height_new, height_next[:, None]], axis=1)
    zonal_new = (1.0 - friction) * zonal - courant * shift_cols(height_new) + rotation * meridional
    merid_new = (
        (1.0 - friction) * meridional
        - courant * (0.5 * (height_ext[:, 2:] - height_ext[:, :-2]))
        - rotation * zonal
    )
    return jnp.stack([height_new, zonal_new, merid_new], axis=1)


def per_device(parent_state, nest_state, offsets):
    members = parent_state.shape[0]
    band_rows = parent_state.shape[2]
    nest_rows = nest_state.shape[2]
    nest_width = nest_state.shape[3]
    span = nest_width // 3
    tile_coarse = nest_rows // 3
    bands = lax.axis_size("band")
    band_index = lax.axis_index("band")
    parent_total = bands * band_rows
    nest_total = bands * nest_rows
    halo = 2 * NSTEPS
    ext_rows = nest_rows + 2 * halo
    rows_off = offsets[:, 0]
    cols_off = offsets[:, 1]
    two = jnp.float32(2.0) / jnp.float32(3.0)
    one = jnp.float32(1.0) / jnp.float32(3.0)

    stepped = parent_step(parent_state)

    colslice = jnp.concatenate(
        [
            lax.dynamic_slice(stepped, (m, 0, 0, cols_off[m] - 1), (1, 3, band_rows, span + 2))
            for m in range(members)
        ],
        axis=0,
    )

    window_cols = jnp.arange(span + 2, dtype=jnp.int32)[:, None]
    west_side = jnp.arange(2, dtype=jnp.int32)[None, :] == 0
    column_weights = (
        jnp.where(west_side & (window_cols == 0), two, 0.0)
        + jnp.where(west_side & (window_cols == 1), one, 0.0)
        + jnp.where(~west_side & (window_cols == span), one, 0.0)
        + jnp.where(~west_side & (window_cols == span + 1), two, 0.0)
    )
    strip = jnp.einsum("mflq,qs->mfsl", colslice, column_weights, precision=highest)
    strip = strip.reshape(members * 6, band_rows)

    global_rows = band_index * band_rows + jnp.arange(band_rows, dtype=jnp.int32)
    row_start = rows_off[:, None]
    south_weight = jnp.where(global_rows[None, :] == row_start - 1, two, 0.0) + jnp.where(
        global_rows[None, :] == row_start, one, 0.0
    )
    north_weight = jnp.where(global_rows[None, :] == row_start + span - 1, one, 0.0) + jnp.where(
        global_rows[None, :] == row_start + span, two, 0.0
    )
    row_weights = jnp.stack([south_weight, north_weight], axis=1)
    ends_part = jnp.einsum("msl,mflq->mfsq", row_weights, colslice, precision=highest)

    blocks = strip
    sums = ends_part.reshape(members * 6, span + 2)
    reach = 1
    while reach < bands:
        count = min(4 if reach == 1 else 8, bands // reach)
        payload = jnp.concatenate([blocks, sums], axis=1)
        if reach == 1:
            nest_state, payload = lax.optimization_barrier((nest_state, payload))
        width = blocks.shape[1]
        recvs = [
            lax.ppermute(payload, "band", [(i, (i + k * reach) % bands) for i in range(bands)])
            for k in range(count - 1, 0, -1)
        ]
        blocks = jnp.concatenate([got[:, :width] for got in recvs] + [blocks], axis=1)
        for got in recvs:
            sums = sums + got[:, width:]
        reach *= count
    strip_all = blocks.reshape(members, 3, 2, parent_total)
    held_rows = ((band_index + 1) * band_rows + jnp.arange(parent_total, dtype=jnp.int32)) % parent_total
    ends_full = sums.reshape(members, 3, 2, span + 2)
    inner_weights = interp_matrix(nest_width + 2, span + 2)[1:-1]
    ends = jnp.einsum("jq,mfsq->mfsj", inner_weights, ends_full, precision=highest)

    nest_global = band_index * nest_rows - halo + jnp.arange(ext_rows, dtype=jnp.int32)
    base = (nest_global + 2) // 3
    frac = (nest_global + 2) % 3
    lower = (3 - frac).astype(jnp.float32) / 3.0
    upper = frac.astype(jnp.float32) / 3.0
    first_row = rows_off[:, None] - 1 + base[None, :]
    all_rows = held_rows[None, None, :]
    side_weights = jnp.where(all_rows == first_row[:, :, None], lower[None, :, None], 0.0) + jnp.where(
        all_rows == first_row[:, :, None] + 1, upper[None, :, None], 0.0
    )
    side_ext = jnp.einsum("mkr,mfsr->mfsk", side_weights, strip_all, precision=highest)

    nest_ext = with_halo(nest_state, halo)
    is_south = (nest_global == -1)[None, :, None]
    is_north = (nest_global == nest_total)[None, :, None]

    def fix(field, f):
        return jnp.where(
            is_south,
            ends[:, f, 0][:, None, :],
            jnp.where(is_north, ends[:, f, 1][:, None, :], field),
        )

    def dx(field, f):
        west_col = side_ext[:, f, 0][:, :, None]
        east_col = side_ext[:, f, 1][:, :, None]
        right = jnp.concatenate([field[:, :, 1:], east_col], axis=2)
        left = jnp.concatenate([west_col, field[:, :, :-1]], axis=2)
        return 0.5 * (right - left)

    def dy(field):
        zero = jnp.zeros_like(field[:, :1])
        up = jnp.concatenate([field[:, 1:], zero], axis=1)
        down = jnp.concatenate([zero, field[:, :-1]], axis=1)
        return 0.5 * (up - down)

    height, zonal, meridional = (nest_ext[:, 0], nest_ext[:, 1], nest_ext[:, 2])
    for _ in range(NSTEPS):
        zonal_fixed = fix(zonal, 1)
        merid_fixed = fix(meridional, 2)
        height_new = height - courant * (dx(zonal_fixed, 1) + dy(merid_fixed))
        height_fixed = fix(height_new, 0)
        zonal_new = (1.0 - friction) * zonal - courant * dx(height_fixed, 0) + rotation * meridional
        merid_new = (1.0 - friction) * meridional - courant * dy(height_fixed) - rotation * zonal
        height, zonal, meridional = height_new, zonal_new, merid_new
    nest = jnp.stack([height, zonal, meridional], axis=1)[:, :, halo : halo + nest_rows]

    block_cols = (
        jnp.arange(nest_width, dtype=jnp.int32)[:, None] // 3
        == jnp.arange(span, dtype=jnp.int32)[None, :]
    ).astype(jnp.float32)
    col_sums = jnp.einsum("mfrj,jp->mfrp", nest, block_cols, precision=highest)
    coarse = col_sums.reshape(members, 3, tile_coarse, 3, span).sum(axis=3) / 9.0

    shift = (rows_off + tile_coarse - 1) // tile_coarse - 1
    moved = coarse
    step = 1
    while step < bands:
        recv = lax.ppermute(moved, "band", [(i, (i + step) % bands) for i in range(bands)])
        take = ((shift // step) % 2 == 1)[:, None, None, None]
        moved = jnp.where(take, recv, moved)
        step *= 2
    half = bands // 2
    low_half = band_index < half
    pieces = []
    for i in range(3):
        got = []
        for h in range(2):
            pairs = [((2 * p - 1 + i) % bands, p) for p in range(h * half, (h + 1) * half)]
            got.append(lax.ppermute(moved, "band", pairs))
        pieces.append(jnp.where(low_half, got[0], got[1]))
    near = jnp.concatenate(pieces, axis=2)
    lead = tile_coarse * (shift + 1) - rows_off
    patch = jax.vmap(lambda blk, e: lax.dynamic_slice_in_dim(blk, e, band_rows, axis=1))(near, lead)

    relative_rows = global_rows[None, :] - rows_off[:, None]
    covered = (relative_rows >= 0) & (relative_rows < span)
    merged = jnp.where(covered[:, None, :, None], patch, colslice[..., 1 : span + 1])
    parent_out = stepped
    for m in range(members):
        parent_out = lax.dynamic_update_slice(parent_out, merged[m : m + 1], (m, 0, 0, cols_off[m]))
    return (parent_out, nest)


def solution(mesh):
    in_specs = (P("member", None, "band", None), P("member", None, "band", None), P("member", None))
    out_specs = (P("member", None, "band", None), P("member", None, "band", None))
    return jax.shard_map(
        per_device, mesh=mesh, in_specs=in_specs, out_specs=out_specs, check_vma=False
    )
```
